256 devices in a mesh: rows: 128 (over y, x, z), cols: 2 (over core).
Axes of the slice: x: 4, y: 4, z: 8, core: 2. Of those that a mesh axis runs over, the one named last changes fastest.
Arguments:
- matrix: bfloat16 [128, 524288], P('cols', 'rows'), may hold values from -6 to 6
- signs: int32 [524288], P('rows'), may hold values 0 or 1
- samples: int32 [256, 256], replicated, may hold values from 0 to 524287, as said below
- owners: int32 [256, 1], replicated, may hold values from 0 to 127; in each aligned block of 256 rows (0 to 255, 256 to 511, ...) at most 4 rows name the same one
Outputs:
- factors: float32 [512, 128, 128], P('rows', 'cols')
The draws below stay inside these ranges and needn't reach their ends.
Inputs may be any that keep to these rules, and one draw needn't show every extreme that they name: samples[b, q] = s * 4096 + ((q + b) % 128) * 32 + u with s = q // 2 and 0 <= u < 32. `owners`: every index of rows owns at least one block and at most 4; some index owns exactly 4.
All inputs are finite; a program needn't handle non-finite values. No bound on the sum of `signs` on one device may be relied on, other than what follows from the above.
Results may differ from the reference program's by a relative error of at most 0.0003.
Values sent between devices are 32-bit elements; how exact they have to be, the bound alone decides.
No kernel may reach another device: no remote copies, remote signals or barrier semaphores. Data moves between devices by JAX's collectives and lax.ppermute only.
A program may use at most 64 MiB of HBM per device.

```python
import math
import jax
import jax.numpy as jnp
import numpy as np
from jax import lax

HB = 128
SKETCH_ROW_COUNT = 256
CAPB = 4
R_DEV = 4096
M = 524288
COLS = 128
BLOCKS = 256
N_ROWS = 128


def draw_samples(key, part):
    sample_pos = jnp.arange(SKETCH_ROW_COUNT, dtype=jnp.int32)
    block_pos = jnp.arange(BLOCKS, dtype=jnp.int32)
    shard_of = sample_pos // (SKETCH_ROW_COUNT // N_ROWS)
    sub_range = jnp.mod(sample_pos[None, :] + block_pos[:, None], N_ROWS)
    offsets = jax.random.randint(key, (BLOCKS, SKETCH_ROW_COUNT), 0, R_DEV // N_ROWS, dtype=jnp.int32)
    return shard_of[None, :] * R_DEV + sub_range * (R_DEV // N_ROWS) + offsets


def with_ends(array, stream_key, smallest, largest):
    spot = [jax.random.randint(jax.random.fold_in(stream_key, axis), (), 0, length) for axis, length in enumerate(array.shape)]
    main_axis = array.shape.index(max(array.shape))
    neighbour = spot[:main_axis] + [(spot[main_axis] + 1) % array.shape[main_axis]] + spot[main_axis + 1:]
    return array.at[tuple(spot)].set(smallest).at[tuple(neighbour)].set(largest)


def block_levels(rng, dims, shards, low, largest):
    def one(position, parts):
        draws = jax.random.uniform(jax.random.fold_in(jax.random.fold_in(rng, 6), position), (parts,), jnp.float32, low / len(shards), largest / len(shards))
        return jnp.repeat(jnp.exp(draws), dims[position] // parts).reshape((-1,) + (1,) * (len(dims) - position - 1))

    factor_of = one(*shards[0])
    for cut in shards[1:]:
        factor_of = factor_of * one(*cut)
    return factor_of


def shared_out(own_key, own, number, rows, number_of, top, most, skew):
    order = jax.random.permutation(own_key, number_of)
    crowded, usual = load_shares(number_of, rows * top, most, skew, True), load_shares(number_of, rows * top, most, skew, False)
    places = jnp.arange(number_of)

    def named(lengths, turn):
        used = int((lengths > 0).sum())
        fixed = max(1, used // 4)
        moved = fixed + (places - fixed + turn * (used - fixed)) % max(1, number_of - fixed)
        return jnp.zeros((number_of,), jnp.int32).at[order[jnp.where(places < fixed, places, moved)]].set(jnp.asarray(lengths, jnp.int32))

    lengths = jnp.where(number % 4 == 0, named(crowded, number // 4), named(usual, number - number // 4 - 1))
    mixed = jax.random.permutation(jax.random.fold_in(own, 3), number_of)
    source_of, taker = mixed[0:number_of // 2 * 2:2], mixed[1:number_of // 2 * 2:2]
    room = jnp.minimum(lengths[source_of] - 1, most - lengths[taker]) // 2
    room = jnp.where((source_of == order[0]) | (taker == order[0]) | (lengths[taker] == 0), 0, jnp.maximum(room, 0))
    moved = jax.random.randint(jax.random.fold_in(own, 4), (number_of // 2,), 0, 1 << 20) % (room + 1)
    lengths = lengths.at[source_of].add(-moved).at[taker].add(moved)
    items = jnp.searchsorted(jnp.cumsum(lengths), jnp.arange(rows * top), side="right").astype(jnp.int32)
    listing = items.reshape(top, rows).T
    listing = listing[jax.random.permutation(jax.random.fold_in(own, 1), rows)]
    turn = jax.random.randint(jax.random.fold_in(own, 2), (rows, 1), 0, top)
    return jnp.take_along_axis(listing, (jnp.arange(top)[None, :] + turn) % top, axis=1)


def load_shares(amount, total, most, slope, full):
    weights = [(1 << 20) // math.isqrt(standing ** slope) + 1 for standing in range(1, amount + 1)]
    largest = most if full else min(most, max(-(-total // amount), total * weights[0] // sum(weights)))
    least = 1 if total - largest >= amount - 1 else 0
    counts, surplus = [largest] + [least] * (amount - 1), total - largest - least * (amount - 1)
    while surplus > 0:
        movable = [i for i in range(1, amount) if counts[i] < largest] or [i for i in range(1, amount) if counts[i] < most]
        pool, left = sum([weights[i] for i in movable]), surplus
        for i in movable:
            addition = min(most - counts[i], max(1, left * weights[i] // pool), surplus)
            counts[i] = counts[i] + addition
            surplus = surplus - addition
    return np.array(counts)


def centred(own_key, extent, width, limit, pieces=(), kind=jnp.bfloat16):
    result = jax.random.normal(own_key, extent, jnp.float32) * width
    if len(pieces) > 0:
        result = block_levels(own_key, extent, pieces, -0.22, 0.18) * result
    return jnp.clip(result, min=-limit, max=limit).astype(kind)


def setup_inputs(seed: int = 0) -> dict:
    key_of = jax.random.split(jax.random.key(seed), 5)
    matrix = centred(key_of[0], (COLS, M), 1.0, 6.0, ((0, 2), (1, 128)))
    signs = with_ends((jax.random.randint(key_of[1], (M,), 0, 2) < 1).astype(jnp.int32), jax.random.fold_in(key_of[1], 1), 0, 1)
    samples = draw_samples(jax.random.fold_in(key_of[4], 71), 0)
    owners_keys = jax.random.split(jax.random.fold_in(key_of[3], 1), BLOCKS // BLOCKS)
    owners_turns = jax.random.permutation(jax.random.fold_in(key_of[3], 3), BLOCKS // BLOCKS)
    owners = jax.vmap(lambda own, number: shared_out(jax.random.fold_in(key_of[3], 2), own, number, BLOCKS, N_ROWS, 1, CAPB, 2))(owners_keys, owners_turns).reshape((BLOCKS, 1))
    return {"matrix": matrix, "signs": signs, "samples": samples, "owners": owners}


def walsh_sign_matrix(order):
    index_row = jnp.arange(order, dtype=jnp.int32)
    parity = jnp.zeros((order, order), jnp.int32)
    for bit_place in range(order.bit_length() - 1):
        both = jnp.bitwise_and(index_row[:, None], index_row[None, :])
        parity = parity + jnp.bitwise_and(jnp.right_shift(both, bit_place), 1)
    return (1 - 2 * (parity % 2)).astype(jnp.float32)

def reference(matrix, signs, samples, owners):
    flips = (1 - 2 * signs).astype(jnp.bfloat16)
    flipped = (matrix * flips[None, :]).T
    table = walsh_sign_matrix(HB)
    scale = 1.0 / math.sqrt(HB * N_ROWS)
    blocked = flipped.astype(jnp.float32).reshape(M // HB, HB, COLS)
    local_mix = jnp.einsum('ij,bjc->bic', table, blocked, precision=lax.Precision.HIGHEST) * scale
    current = local_mix.reshape(N_ROWS, R_DEV * COLS)
    half_width = 1
    for section_bit in range(N_ROWS.bit_length() - 1):
        shaped = current.reshape(N_ROWS // (2 * half_width), 2, half_width, R_DEV * COLS)
        upper_part = shaped[:, 0]
        lower_part = shaped[:, 1]
        current = jnp.stack([upper_part + lower_part, upper_part - lower_part], axis=1).reshape(N_ROWS, R_DEV * COLS)
        half_width = half_width * 2
    mixed = current.reshape(M, COLS)
    selected_rows = mixed[samples]
    gram_product = jnp.einsum('eym,eyd->emd', selected_rows, selected_rows, precision=lax.Precision.HIGHEST) / SKETCH_ROW_COUNT
    lower_factor = jnp.linalg.cholesky(gram_product)
    upper = jnp.swapaxes(lower_factor, -1, -2)
    owner_list = owners[:, 0]
    positions = jnp.arange(BLOCKS, dtype=jnp.int32)
    preceding_rows = jnp.logical_and(owner_list[None, :] == owner_list[:, None], positions[None, :] < positions[:, None])
    ranks = lax.optimization_barrier(jnp.sum(preceding_rows.astype(jnp.int32), axis=1))
    slots = owner_list * CAPB + ranks
    factors = jnp.zeros((N_ROWS * CAPB, COLS, COLS), jnp.float32).at[slots].set(upper)
    return factors
```

```python
import math

import jax
import jax.numpy as jnp
from jax import lax
from jax.sharding import PartitionSpec as P

HB = 128
SKETCH_ROW_COUNT = 256
CAPB = 4


def walsh_sign_matrix(order):
    index_row = jnp.arange(order, dtype=jnp.int32)
    parity = jnp.zeros((order, order), jnp.int32)
    for bit_place in range(order.bit_length() - 1):
        both = jnp.bitwise_and(index_row[:, None], index_row[None, :])
        parity = parity + jnp.bitwise_and(jnp.right_shift(both, bit_place), 1)
    return (1 - 2 * (parity % 2)).astype(jnp.float32)


def per_device(matrix, signs, samples, owners):
    slab_width = matrix.shape[0]
    shard_rows = matrix.shape[1]
    row_devices = lax.axis_size("rows")
    processor_number = lax.axis_index("rows")
    sub_rows = shard_rows // row_devices
    flips = (1 - 2 * signs).astype(jnp.bfloat16)
    flipped = matrix * flips[None, :]
    table = walsh_sign_matrix(HB).astype(jnp.bfloat16)
    scale = 1.0 / math.sqrt(HB * row_devices)
    local_mix = jnp.einsum(
        "huj,cbj->bhuc",
        table.reshape(HB // sub_rows, sub_rows, HB),
        flipped.reshape(slab_width, shard_rows // HB, HB),
        preferred_element_type=jnp.float32,
    )
    outgoing = local_mix.reshape(row_devices, sub_rows, slab_width) * scale
    received = lax.all_to_all(outgoing, "rows", split_axis=0, concat_axis=0, tiled=True)
    across = walsh_sign_matrix(row_devices)
    mixed = jnp.einsum(
        "st,tuc->suc", across, received, precision=lax.Precision.HIGHEST
    ).reshape(row_devices * sub_rows, slab_width)

    block_total = samples.shape[0]
    block_ids = jnp.arange(block_total, dtype=jnp.int32)
    first_q = jnp.mod(processor_number - block_ids, row_devices)
    picks = jnp.stack([first_q, first_q + row_devices], axis=1)
    sample_values = jnp.take_along_axis(samples, picks, axis=1)
    shard_of = picks // (samples.shape[1] // row_devices)
    offsets = sample_values - shard_of * shard_rows - processor_number * sub_rows
    chosen = jnp.take(mixed, shard_of * sub_rows + offsets, axis=0)

    owner_list = owners[:, 0]
    preceding_rows = jnp.logical_and(
        owner_list[None, :] == owner_list[:, None], block_ids[None, :] < block_ids[:, None]
    )
    ranks = jnp.sum(preceding_rows.astype(jnp.int32), axis=1)
    slots = owner_list * CAPB + ranks
    placing = (jnp.arange(row_devices * CAPB, dtype=jnp.int32)[:, None] == slots[None, :]).astype(
        jnp.float32
    )
    bundled = jnp.einsum("kb,bps->kps", placing, chosen, precision=lax.Precision.HIGHEST)
    bundled = bundled.reshape(row_devices, CAPB, 2, slab_width)
    arriving = lax.all_to_all(bundled, "rows", split_axis=0, concat_axis=0, tiled=True)
    received_rows = jnp.transpose(arriving, (1, 0, 2, 3)).reshape(CAPB, row_devices * 2, slab_width)
    whole_rows = lax.all_gather(received_rows, "cols", axis=2, tiled=True)
    window_width = whole_rows.shape[2]
    gram_product = (
        jnp.einsum("sqi,sqk->sik", whole_rows, whole_rows, precision=lax.Precision.HIGHEST)
        / SKETCH_ROW_COUNT
    )
    owned_total = jnp.sum((owner_list == processor_number).astype(jnp.int32))
    live = jnp.arange(CAPB, dtype=jnp.int32) < owned_total
    identity = jnp.eye(window_width, dtype=jnp.float32)
    safe = jnp.where(live[:, None, None], gram_product, identity[None, :, :])
    upper = jnp.swapaxes(jnp.linalg.cholesky(safe), -1, -2)
    upper = jnp.where(live[:, None, None], upper, jnp.zeros_like(upper))
    column_start = lax.axis_index("cols") * slab_width
    return lax.dynamic_slice_in_dim(upper, column_start, slab_width, 1)


def solution(mesh):
    in_specs = (P("cols", "rows"), P("rows"), P(), P())
    out_specs = P("rows", "cols", None)
    return jax.shard_map(
        per_device, mesh=mesh, in_specs=in_specs, out_specs=out_specs, check_vma=False
    )
```

```python
import math

import jax
import jax.numpy as jnp
from jax import lax
from jax.experimental import pallas as pl
from jax.experimental.pallas import tpu as pltpu
from jax.sharding import PartitionSpec as P

HB = 128
SKETCH_ROW_COUNT = 256
CAPB = 4

PANEL = 8


def cholesky_kernel(gram_ref, out_ref, work_ref):
    blocks, order, _ = gram_ref.shape
    work_ref[...] = gram_ref[...]
    lane = lax.broadcasted_iota(jnp.int32, (blocks, 1, order), 2)
    lane_panel = lax.broadcasted_iota(jnp.int32, (blocks, PANEL, order), 2)
    sub_panel = lax.broadcasted_iota(jnp.int32, (blocks, PANEL, order), 1)
    for p in range(order // PANEL):
        base = p * PANEL
        panel = work_ref[:, base:base + PANEL, :]
        for jj in range(PANEL):
            j = base + jj
            row = panel[:, jj:jj + 1, :]
            pivot = row[:, :, j:j + 1]
            r = jnp.where(lane >= j, row / jnp.sqrt(pivot), 0.0)
            spread = jnp.broadcast_to(r, (blocks, PANEL, order))
            col = jnp.sum(jnp.where(lane_panel == base + sub_panel, spread, 0.0), axis=2, keepdims=True)
            col = jnp.where(sub_panel[:, :, :1] > jj, col, 0.0)
            panel = panel - col * spread
            panel = jnp.where(sub_panel == jj, spread, panel)
        out_ref[:, base:base + PANEL, :] = panel
        if p + 1 < order // PANEL:
            for b in range(blocks):
                update = lax.dot_general(
                    panel[b], panel[b], (((0,), (0,)), ((), ())),
                    precision=lax.Precision.HIGHEST, preferred_element_type=jnp.float32,
                )
                work_ref[b, base + PANEL:, :] = work_ref[b, base + PANEL:, :] - update[base + PANEL:, :]


def cholesky_upper(gram):
    blocks, order, _ = gram.shape
    return pl.pallas_call(
        cholesky_kernel,
        out_shape=jax.ShapeDtypeStruct(gram.shape, jnp.float32),
        in_specs=[pl.BlockSpec(memory_space=pltpu.VMEM)],
        out_specs=pl.BlockSpec(memory_space=pltpu.VMEM),
        scratch_shapes=[pltpu.VMEM(gram.shape, jnp.float32)],
    )(gram)


def walsh_sign_matrix(order):
    index_row = jnp.arange(order, dtype=jnp.int32)
    parity = jnp.zeros((order, order), jnp.int32)
    for bit_place in range(order.bit_length() - 1):
        both = jnp.bitwise_and(index_row[:, None], index_row[None, :])
        parity = parity + jnp.bitwise_and(jnp.right_shift(both, bit_place), 1)
    return (1 - 2 * (parity % 2)).astype(jnp.float32)


def per_device(matrix, signs, samples, owners):
    slab_width = matrix.shape[0]
    shard_rows = matrix.shape[1]
    row_devices = lax.axis_size("rows")
    processor_number = lax.axis_index("rows")
    sub_rows = shard_rows // row_devices
    flips = (1 - 2 * signs).astype(jnp.bfloat16)
    flipped = matrix * flips[None, :]
    table = walsh_sign_matrix(HB).astype(jnp.bfloat16)
    scale = 1.0 / math.sqrt(HB * row_devices)
    local_mix = jnp.einsum(
        "huj,cbj->bhuc",
        table.reshape(HB // sub_rows, sub_rows, HB),
        flipped.reshape(slab_width, shard_rows // HB, HB),
        preferred_element_type=jnp.float32,
    )
    outgoing = local_mix.reshape(row_devices, sub_rows, slab_width) * scale
    received = lax.all_to_all(outgoing, "rows", split_axis=0, concat_axis=0, tiled=True)
    across = walsh_sign_matrix(row_devices)
    mixed = jnp.einsum(
        "st,tuc->suc", across, received, precision=lax.Precision.HIGHEST
    ).reshape(row_devices * sub_rows, slab_width)

    block_total = samples.shape[0]
    block_ids = jnp.arange(block_total, dtype=jnp.int32)
    first_q = jnp.mod(processor_number - block_ids, row_devices)
    picks = jnp.stack([first_q, first_q + row_devices], axis=1)
    sample_values = jnp.take_along_axis(samples, picks, axis=1)
    shard_of = picks // (samples.shape[1] // row_devices)
    offsets = sample_values - shard_of * shard_rows - processor_number * sub_rows
    chosen = jnp.take(mixed, shard_of * sub_rows + offsets, axis=0)

    owner_list = owners[:, 0]
    preceding_rows = jnp.logical_and(
        owner_list[None, :] == owner_list[:, None], block_ids[None, :] < block_ids[:, None]
    )
    ranks = jnp.sum(preceding_rows.astype(jnp.int32), axis=1)
    slots = owner_list * CAPB + ranks
    placing = (jnp.arange(row_devices * CAPB, dtype=jnp.int32)[:, None] == slots[None, :]).astype(
        jnp.float32
    )
    bundled = jnp.einsum("kb,bps->kps", placing, chosen, precision=lax.Precision.HIGHEST)
    bundled = bundled.reshape(row_devices, CAPB, 2, slab_width)
    arriving = lax.all_to_all(bundled, "rows", split_axis=0, concat_axis=0, tiled=True)
    received_rows = jnp.transpose(arriving, (1, 0, 2, 3)).reshape(CAPB, row_devices * 2, slab_width)
    whole_rows = lax.all_gather(received_rows, "cols", axis=2, tiled=True)
    window_width = whole_rows.shape[2]
    gram_product = (
        jnp.einsum("sqi,sqk->sik", whole_rows, whole_rows, precision=lax.Precision.HIGHEST)
        / SKETCH_ROW_COUNT
    )
    owned_total = jnp.sum((owner_list == processor_number).astype(jnp.int32))
    live = jnp.arange(CAPB, dtype=jnp.int32) < owned_total
    identity = jnp.eye(window_width, dtype=jnp.float32)
    safe = jnp.where(live[:, None, None], gram_product, identity[None, :, :])
    upper = cholesky_upper(safe)
    upper = jnp.where(live[:, None, None], upper, jnp.zeros_like(upper))
    column_start = lax.axis_index("cols") * slab_width
    return lax.dynamic_slice_in_dim(upper, column_start, slab_width, 1)


def solution(mesh):
    in_specs = (P("cols", "rows"), P("rows"), P(), P())
    out_specs = P("rows", "cols", None)
    return jax.shard_map(
        per_device, mesh=mesh, in_specs=in_specs, out_specs=out_specs, check_vma=False
    )
```

```python
import math

import jax
import jax.numpy as jnp
from jax import lax
from jax.experimental import pallas as pl
from jax.experimental.pallas import tpu as pltpu
from jax.sharding import PartitionSpec as P

HB = 128
SKETCH_ROW_COUNT = 256
CAPB = 4

PANEL = 32


def cholesky_kernel(gram_ref, out_ref, work_ref):
    blocks, order, _ = gram_ref.shape
    work_ref[...] = gram_ref[...]
    lane = lax.broadcasted_iota(jnp.int32, (blocks, 1, order), 2)
    sub_panel = lax.broadcasted_iota(jnp.int32, (blocks, PANEL, order), 1)
    sub_col = lax.broadcasted_iota(jnp.int32, (blocks, PANEL, 1), 1)
    for p in range(order // PANEL):
        base = p * PANEL
        panel = work_ref[:, base:base + PANEL, :]
        for jj in range(PANEL):
            j = base + jj
            row = panel[:, jj:jj + 1, :]
            column = panel[:, :, j:j + 1]
            inverse_root = lax.rsqrt(column[:, jj:jj + 1, :])
            factor_row = jnp.where(lane >= j, row * inverse_root, 0.0)
            factor_column = jnp.where(sub_col > jj, column * inverse_root, 0.0)
            panel = panel - factor_column * factor_row
            panel = jnp.where(sub_panel == jj, factor_row, panel)
        out_ref[:, base:base + PANEL, :] = panel
        if p + 1 < order // PANEL:
            for b in range(blocks):
                update = lax.dot_general(
                    panel[b], panel[b], (((0,), (0,)), ((), ())),
                    precision=lax.Precision.HIGHEST, preferred_element_type=jnp.float32,
                )
                work_ref[b, base + PANEL:, :] = work_ref[b, base + PANEL:, :] - update[base + PANEL:, :]


def cholesky_upper(gram):
    blocks, order, _ = gram.shape
    return pl.pallas_call(
        cholesky_kernel,
        out_shape=jax.ShapeDtypeStruct(gram.shape, jnp.float32),
        in_specs=[pl.BlockSpec(memory_space=pltpu.VMEM)],
        out_specs=pl.BlockSpec(memory_space=pltpu.VMEM),
        scratch_shapes=[pltpu.VMEM(gram.shape, jnp.float32)],
    )(gram)


def walsh_sign_matrix(order):
    index_row = jnp.arange(order, dtype=jnp.int32)
    parity = jnp.zeros((order, order), jnp.int32)
    for bit_place in range(order.bit_length() - 1):
        both = jnp.bitwise_and(index_row[:, None], index_row[None, :])
        parity = parity + jnp.bitwise_and(jnp.right_shift(both, bit_place), 1)
    return (1 - 2 * (parity % 2)).astype(jnp.float32)


def per_device(matrix, signs, samples, owners):
    slab_width = matrix.shape[0]
    shard_rows = matrix.shape[1]
    row_devices = lax.axis_size("rows")
    processor_number = lax.axis_index("rows")
    sub_rows = shard_rows // row_devices
    flips = (1 - 2 * signs).astype(jnp.bfloat16)
    flipped = matrix * flips[None, :]
    table = walsh_sign_matrix(HB).astype(jnp.bfloat16)
    scale = 1.0 / math.sqrt(HB * row_devices)
    local_mix = jnp.einsum(
        "huj,cbj->bhuc",
        table.reshape(HB // sub_rows, sub_rows, HB),
        flipped.reshape(slab_width, shard_rows // HB, HB),
        preferred_element_type=jnp.float32,
    )
    outgoing = local_mix.reshape(row_devices, sub_rows * slab_width // 128, 128) * scale
    received = lax.all_to_all(outgoing, "rows", split_axis=0, concat_axis=0, tiled=True)
    received = received.reshape(row_devices, sub_rows, slab_width)
    across = walsh_sign_matrix(row_devices)
    mixed = jnp.einsum(
        "st,tuc->suc", across, received, precision=lax.Precision.HIGHEST
    ).reshape(row_devices * sub_rows, slab_width)

    block_total = samples.shape[0]
    block_ids = jnp.arange(block_total, dtype=jnp.int32)
    first_q = jnp.mod(processor_number - block_ids, row_devices)
    picks = jnp.stack([first_q, first_q + row_devices], axis=1)
    sample_values = jnp.take_along_axis(samples, picks, axis=1)
    shard_of = picks // (samples.shape[1] // row_devices)
    offsets = sample_values - shard_of * shard_rows - processor_number * sub_rows
    chosen = jnp.take(mixed, shard_of * sub_rows + offsets, axis=0)

    owner_list = owners[:, 0]
    preceding_rows = jnp.logical_and(
        owner_list[None, :] == owner_list[:, None], block_ids[None, :] < block_ids[:, None]
    )
    ranks = jnp.sum(preceding_rows.astype(jnp.int32), axis=1)
    slots = owner_list * CAPB + ranks
    placing = (jnp.arange(row_devices * CAPB, dtype=jnp.int32)[:, None] == slots[None, :]).astype(
        jnp.float32
    )
    bundled = jnp.einsum("kb,bps->kps", placing, chosen, precision=lax.Precision.HIGHEST)
    bundled = bundled.reshape(row_devices, CAPB, 2, slab_width)
    arriving = lax.all_to_all(bundled, "rows", split_axis=0, concat_axis=0, tiled=True)
    received_rows = jnp.transpose(arriving, (1, 0, 2, 3)).reshape(CAPB, row_devices * 2, slab_width)
    whole_rows = lax.all_gather(received_rows, "cols", axis=2, tiled=True)
    window_width = whole_rows.shape[2]
    gram_product = (
        jnp.einsum("sqi,sqk->sik", whole_rows, whole_rows, precision=lax.Precision.HIGHEST)
        / SKETCH_ROW_COUNT
    )
    owned_total = jnp.sum((owner_list == processor_number).astype(jnp.int32))
    live = jnp.arange(CAPB, dtype=jnp.int32) < owned_total
    identity = jnp.eye(window_width, dtype=jnp.float32)
    safe = jnp.where(live[:, None, None], gram_product, identity[None, :, :])
    upper = cholesky_upper(safe)
    upper = jnp.where(live[:, None, None], upper, jnp.zeros_like(upper))
    column_start = lax.axis_index("cols") * slab_width
    return lax.dynamic_slice_in_dim(upper, column_start, slab_width, 1)


def solution(mesh):
    in_specs = (P("cols", "rows"), P("rows"), P(), P())
    out_specs = P("rows", "cols", None)
    return jax.shard_map(
        per_device, mesh=mesh, in_specs=in_specs, out_specs=out_specs, check_vma=False
    )
```

```python
import math

import jax
import jax.numpy as jnp
from jax import lax
from jax.experimental import pallas as pl
from jax.experimental.pallas import tpu as pltpu
from jax.sharding import PartitionSpec as P

HB = 128
SKETCH_ROW_COUNT = 256
CAPB = 4

PANEL = 32


def cholesky_kernel(gram_ref, out_ref, work_ref):
    blocks, order, _ = gram_ref.shape
    work_ref[...] = gram_ref[...]
    lane = lax.broadcasted_iota(jnp.int32, (blocks, 1, order), 2)
    sub_panel = lax.broadcasted_iota(jnp.int32, (blocks, PANEL, order), 1)
    sub_col = lax.broadcasted_iota(jnp.int32, (blocks, PANEL, 1), 1)
    for p in range(order // PANEL):
        base = p * PANEL
        panel = work_ref[:, base:base + PANEL, :]
        for jj in range(PANEL):
            j = base + jj
            row = panel[:, jj:jj + 1, :]
            column = panel[:, :, j:j + 1]
            inverse_root = lax.rsqrt(column[:, jj:jj + 1, :])
            factor_row = jnp.where(lane >= j, row * inverse_root, 0.0)
            factor_column = jnp.where(sub_col > jj, column * inverse_root, 0.0)
            panel = panel - factor_column * factor_row
            panel = jnp.where(sub_panel == jj, factor_row, panel)
        out_ref[:, base:base + PANEL, :] = panel
        if p + 1 < order // PANEL:
            for b in range(blocks):
                update = lax.dot_general(
                    panel[b], panel[b], (((0,), (0,)), ((), ())),
                    precision=lax.Precision.HIGHEST, preferred_element_type=jnp.float32,
                )
                work_ref[b, base + PANEL:, :] = work_ref[b, base + PANEL:, :] - update[base + PANEL:, :]


def cholesky_upper(gram):
    blocks, order, _ = gram.shape
    return pl.pallas_call(
        cholesky_kernel,
        out_shape=jax.ShapeDtypeStruct(gram.shape, jnp.float32),
        in_specs=[pl.BlockSpec(memory_space=pltpu.VMEM)],
        out_specs=pl.BlockSpec(memory_space=pltpu.VMEM),
        scratch_shapes=[pltpu.VMEM(gram.shape, jnp.float32)],
    )(gram)


def local_mix_kernel(matrix_ref, flips_ref, table_ref, out_ref):
    slab_width = matrix_ref.shape[0]
    groups = table_ref.shape[1] // out_ref.shape[1]

    def body(blk, carry):
        start = pl.multiple_of(blk * HB, HB)
        flipped = matrix_ref[:, pl.ds(start, HB)] * flips_ref[:, pl.ds(start, HB)]
        for parity in range(2):
            mixed = lax.dot_general(
                table_ref[parity], flipped, (((1,), (1,)), ((), ())),
                preferred_element_type=jnp.float32,
            )
            for h in range(groups):
                rows = out_ref.shape[1]
                out_ref[blk * groups + h, :, parity * slab_width:(parity + 1) * slab_width] = (
                    mixed[h * rows:(h + 1) * rows, :]
                )
        return carry

    lax.fori_loop(0, matrix_ref.shape[1] // HB, body, 0)


def local_mix(matrix, flips, table, row_devices):
    slab_width, shard_rows = matrix.shape
    sub_rows = shard_rows // row_devices
    return pl.pallas_call(
        local_mix_kernel,
        out_shape=jax.ShapeDtypeStruct((row_devices, sub_rows // 2, 2 * slab_width), jnp.float32),
        in_specs=[pl.BlockSpec(memory_space=pltpu.VMEM)] * 3,
        out_specs=pl.BlockSpec(memory_space=pltpu.VMEM),
    )(matrix, flips, table)


def walsh_sign_matrix(order):
    index_row = jnp.arange(order, dtype=jnp.int32)
    parity = jnp.zeros((order, order), jnp.int32)
    for bit_place in range(order.bit_length() - 1):
        both = jnp.bitwise_and(index_row[:, None], index_row[None, :])
        parity = parity + jnp.bitwise_and(jnp.right_shift(both, bit_place), 1)
    return (1 - 2 * (parity % 2)).astype(jnp.float32)


def per_device(matrix, signs, samples, owners):
    slab_width = matrix.shape[0]
    shard_rows = matrix.shape[1]
    row_devices = lax.axis_size("rows")
    processor_number = lax.axis_index("rows")
    sub_rows = shard_rows // row_devices
    flips = (1 - 2 * signs).astype(jnp.bfloat16).reshape(1, shard_rows)
    scale = 1.0 / math.sqrt(HB * row_devices)
    table = (walsh_sign_matrix(HB) * scale).astype(jnp.bfloat16)
    table = table.reshape(HB // 2, 2, HB).transpose(1, 0, 2)
    outgoing = local_mix(matrix, flips, table, row_devices)
    received = lax.all_to_all(outgoing, "rows", split_axis=0, concat_axis=0, tiled=True)
    across = walsh_sign_matrix(row_devices)
    mixed = jnp.einsum(
        "st,tvl->svl", across, received, precision=lax.Precision.HIGHEST
    ).reshape(row_devices * sub_rows // 2, 2 * slab_width)

    block_total = samples.shape[0]
    block_ids = jnp.arange(block_total, dtype=jnp.int32)
    first_q = jnp.mod(processor_number - block_ids, row_devices)
    picks = jnp.stack([first_q, first_q + row_devices], axis=1)
    sample_values = jnp.take_along_axis(samples, picks, axis=1)
    shard_of = picks // (samples.shape[1] // row_devices)
    offsets = sample_values - shard_of * shard_rows - processor_number * sub_rows
    both_halves = jnp.take(mixed, shard_of * (sub_rows // 2) + offsets // 2, axis=0)
    chosen = jnp.where(
        (offsets % 2 == 1)[:, :, None], both_halves[:, :, slab_width:], both_halves[:, :, :slab_width]
    )

    owner_list = owners[:, 0]
    preceding_rows = jnp.logical_and(
        owner_list[None, :] == owner_list[:, None], block_ids[None, :] < block_ids[:, None]
    )
    ranks = jnp.sum(preceding_rows.astype(jnp.int32), axis=1)
    slots = owner_list * CAPB + ranks
    placing = (jnp.arange(row_devices * CAPB, dtype=jnp.int32)[:, None] == slots[None, :]).astype(
        jnp.float32
    )
    bundled = jnp.einsum("kb,bps->kps", placing, chosen, precision=lax.Precision.HIGHEST)
    bundled = bundled.reshape(row_devices, CAPB, 2, slab_width)
    arriving = lax.all_to_all(bundled, "rows", split_axis=0, concat_axis=0, tiled=True)
    received_rows = jnp.transpose(arriving, (1, 0, 2, 3)).reshape(CAPB, row_devices * 2, slab_width)
    whole_rows = lax.all_gather(received_rows, "cols", axis=2, tiled=True)
    window_width = whole_rows.shape[2]
    gram_product = (
        jnp.einsum("sqi,sqk->sik", whole_rows, whole_rows, precision=lax.Precision.HIGHEST)
        / SKETCH_ROW_COUNT
    )
    owned_total = jnp.sum((owner_list == processor_number).astype(jnp.int32))
    live = jnp.arange(CAPB, dtype=jnp.int32) < owned_total
    identity = jnp.eye(window_width, dtype=jnp.float32)
    safe = jnp.where(live[:, None, None], gram_product, identity[None, :, :])
    upper = cholesky_upper(safe)
    upper = jnp.where(live[:, None, None], upper, jnp.zeros_like(upper))
    column_start = lax.axis_index("cols") * slab_width
    return lax.dynamic_slice_in_dim(upper, column_start, slab_width, 1)


def solution(mesh):
    in_specs = (P("cols", "rows"), P("rows"), P(), P())
    out_specs = P("rows", "cols", None)
    return jax.shard_map(
        per_device, mesh=mesh, in_specs=in_specs, out_specs=out_specs, check_vma=False
    )
```

```python
import math

import jax
import numpy as np
import jax.numpy as jnp
from jax import lax
from jax.experimental import pallas as pl
from jax.experimental.pallas import tpu as pltpu
from jax.sharding import PartitionSpec as P

HB = 128
SKETCH_ROW_COUNT = 256
CAPB = 4

PANEL = 32


def cholesky_kernel(gram_ref, out_ref, work_ref):
    blocks, order, _ = gram_ref.shape
    work_ref[...] = gram_ref[...]
    lane = lax.broadcasted_iota(jnp.int32, (blocks, 1, order), 2)
    sub_panel = lax.broadcasted_iota(jnp.int32, (blocks, PANEL, order), 1)
    sub_col = lax.broadcasted_iota(jnp.int32, (blocks, PANEL, 1), 1)
    for p in range(order // PANEL):
        base = p * PANEL
        panel = work_ref[:, base:base + PANEL, :]
        for jj in range(PANEL):
            j = base + jj
            row = panel[:, jj:jj + 1, :]
            column = panel[:, :, j:j + 1]
            inverse_root = lax.rsqrt(column[:, jj:jj + 1, :])
            factor_row = jnp.where(lane >= j, row * inverse_root, 0.0)
            factor_column = jnp.where(sub_col > jj, column * inverse_root, 0.0)
            panel = panel - factor_column * factor_row
            panel = jnp.where(sub_panel == jj, factor_row, panel)
        out_ref[:, base:base + PANEL, :] = panel
        if p + 1 < order // PANEL:
            for b in range(blocks):
                update = lax.dot_general(
                    panel[b], panel[b], (((0,), (0,)), ((), ())),
                    precision=lax.Precision.HIGHEST, preferred_element_type=jnp.float32,
                )
                work_ref[b, base + PANEL:, :] = work_ref[b, base + PANEL:, :] - update[base + PANEL:, :]


def cholesky_upper(gram):
    blocks, order, _ = gram.shape
    return pl.pallas_call(
        cholesky_kernel,
        out_shape=jax.ShapeDtypeStruct(gram.shape, jnp.float32),
        in_specs=[pl.BlockSpec(memory_space=pltpu.VMEM)],
        out_specs=pl.BlockSpec(memory_space=pltpu.VMEM),
        scratch_shapes=[pltpu.VMEM(gram.shape, jnp.float32)],
    )(gram)


def local_mix_kernel(matrix_ref, signs_ref, table_ref, out_ref):
    slab_width = matrix_ref.shape[0]
    rows = out_ref.shape[1]
    groups = table_ref.shape[1] // rows

    def body(blk, carry):
        start = pl.multiple_of(blk * HB, HB)
        flips = (1 - 2 * signs_ref[:, pl.ds(start, HB)]).astype(jnp.float32)
        flipped = (matrix_ref[:, pl.ds(start, HB)].astype(jnp.float32) * flips).astype(jnp.bfloat16)
        for parity in range(2):
            mixed = lax.dot_general(
                table_ref[parity], flipped, (((1,), (1,)), ((), ())),
                preferred_element_type=jnp.float32,
            )
            for h in range(groups):
                out_ref[blk * groups + h, :, parity * slab_width:(parity + 1) * slab_width] = (
                    mixed[h * rows:(h + 1) * rows, :]
                )
        return carry

    lax.fori_loop(0, matrix_ref.shape[1] // HB, body, 0, unroll=True)


def local_mix(matrix, signs, table, row_devices):
    slab_width, shard_rows = matrix.shape
    sub_rows = shard_rows // row_devices
    return pl.pallas_call(
        local_mix_kernel,
        out_shape=jax.ShapeDtypeStruct((row_devices, sub_rows // 2, 2 * slab_width), jnp.float32),
        in_specs=[pl.BlockSpec(memory_space=pltpu.VMEM)] * 3,
        out_specs=pl.BlockSpec(memory_space=pltpu.VMEM),
    )(matrix, signs, table)


def walsh_sign_matrix(order):
    index_row = np.arange(order)
    parity = np.zeros((order, order), np.int64)
    for bit_place in range(order.bit_length() - 1):
        both = np.bitwise_and(index_row[:, None], index_row[None, :])
        parity = parity + np.bitwise_and(np.right_shift(both, bit_place), 1)
    return (1 - 2 * (parity % 2)).astype(np.float32)


def per_device(matrix, signs, samples, owners):
    slab_width = matrix.shape[0]
    shard_rows = matrix.shape[1]
    row_devices = lax.axis_size("rows")
    processor_number = lax.axis_index("rows")
    sub_rows = shard_rows // row_devices
    scale = 1.0 / math.sqrt(HB * row_devices)
    table = (walsh_sign_matrix(HB) * scale).reshape(HB // 2, 2, HB).transpose(1, 0, 2)
    outgoing = local_mix(matrix, signs.reshape(1, shard_rows), jnp.asarray(table, jnp.bfloat16), row_devices)
    received = lax.all_to_all(outgoing, "rows", split_axis=0, concat_axis=0, tiled=True)
    across = jnp.asarray(walsh_sign_matrix(row_devices))
    mixed = jnp.einsum(
        "st,tvl->svl", across, received, precision=lax.Precision.HIGHEST
    ).reshape(row_devices * sub_rows // 2, 2 * slab_width)

    block_total = samples.shape[0]
    block_ids = jnp.arange(block_total, dtype=jnp.int32)
    first_q = jnp.mod(processor_number - block_ids, row_devices)
    picks = jnp.stack([first_q, first_q + row_devices], axis=1)
    sample_values = jnp.take_along_axis(samples, picks, axis=1)
    shard_of = picks // (samples.shape[1] // row_devices)
    offsets = sample_values - shard_of * shard_rows - processor_number * sub_rows
    both_halves = jnp.take(mixed, shard_of * (sub_rows // 2) + offsets // 2, axis=0)
    chosen = jnp.where(
        (offsets % 2 == 1)[:, :, None], both_halves[:, :, slab_width:], both_halves[:, :, :slab_width]
    )

    owner_list = owners[:, 0]
    preceding_rows = jnp.logical_and(
        owner_list[None, :] == owner_list[:, None], block_ids[None, :] < block_ids[:, None]
    )
    ranks = jnp.sum(preceding_rows.astype(jnp.int32), axis=1)
    slots = owner_list * CAPB + ranks
    placing = (jnp.arange(row_devices * CAPB, dtype=jnp.int32)[:, None] == slots[None, :]).astype(
        jnp.float32
    )
    bundled = jnp.einsum("kb,bps->kps", placing, chosen, precision=lax.Precision.HIGHEST)
    bundled = bundled.reshape(row_devices, CAPB, 2, slab_width)
    arriving = lax.all_to_all(bundled, "rows", split_axis=0, concat_axis=0, tiled=True)
    received_rows = jnp.transpose(arriving, (1, 0, 2, 3)).reshape(CAPB, row_devices * 2, slab_width)
    whole_rows = lax.all_gather(received_rows, "cols", axis=2, tiled=True)
    window_width = whole_rows.shape[2]
    gram_product = (
        jnp.einsum("sqi,sqk->sik", whole_rows, whole_rows, precision=lax.Precision.HIGHEST)
        / SKETCH_ROW_COUNT
    )
    owned_total = jnp.sum((owner_list == processor_number).astype(jnp.int32))
    live = jnp.arange(CAPB, dtype=jnp.int32) < owned_total
    identity = jnp.eye(window_width, dtype=jnp.float32)
    safe = jnp.where(live[:, None, None], gram_product, identity[None, :, :])
    upper = cholesky_upper(safe)
    upper = jnp.where(live[:, None, None], upper, jnp.zeros_like(upper))
    column_start = lax.axis_index("cols") * slab_width
    return lax.dynamic_slice_in_dim(upper, column_start, slab_width, 1)


def solution(mesh):
    in_specs = (P("cols", "rows"), P("rows"), P(), P())
    out_specs = P("rows", "cols", None)
    return jax.shard_map(
        per_device, mesh=mesh, in_specs=in_specs, out_specs=out_specs, check_vma=False
    )
```

```python
import math

import jax
import numpy as np
import jax.numpy as jnp
from jax import lax
from jax.experimental import pallas as pl
from jax.experimental.pallas import tpu as pltpu
from jax.sharding import PartitionSpec as P

HB = 128
SKETCH_ROW_COUNT = 256
CAPB = 4

PANEL = 32


def cholesky_kernel(column_ref, rows_ref, live_ref, out_ref, work_ref):
    blocks, samples, order = rows_ref.shape
    for b in range(blocks):
        gram = lax.dot_general(
            rows_ref[b], rows_ref[b], (((0,), (0,)), ((), ())),
            precision=lax.Precision.HIGHEST, preferred_element_type=jnp.float32,
        ) / samples
        diagonal = (
            lax.broadcasted_iota(jnp.int32, (order, order), 0)
            == lax.broadcasted_iota(jnp.int32, (order, order), 1)
        )
        identity = jnp.where(diagonal, 1.0, 0.0)
        work_ref[b] = jnp.where(live_ref[b] > 0.0, gram, identity)
    lane = lax.broadcasted_iota(jnp.int32, (blocks, 1, order), 2)
    sub_panel = lax.broadcasted_iota(jnp.int32, (blocks, PANEL, order), 1)
    sub_col = lax.broadcasted_iota(jnp.int32, (blocks, PANEL, 1), 1)
    for p in range(order // PANEL):
        base = p * PANEL
        panel = work_ref[:, base:base + PANEL, :]
        for jj in range(PANEL):
            j = base + jj
            row = panel[:, jj:jj + 1, :]
            column = panel[:, :, j:j + 1]
            inverse_root = lax.rsqrt(column[:, jj:jj + 1, :])
            factor_row = jnp.where(lane >= j, row * inverse_root, 0.0)
            factor_column = jnp.where(sub_col > jj, column * inverse_root, 0.0)
            panel = panel - factor_column * factor_row
            panel = jnp.where(sub_panel == jj, factor_row, panel)
        if p + 1 < order // PANEL:
            for b in range(blocks):
                update = lax.dot_general(
                    panel[b], panel[b], (((0,), (0,)), ((), ())),
                    precision=lax.Precision.HIGHEST, preferred_element_type=jnp.float32,
                )
                work_ref[b, base + PANEL:, :] = work_ref[b, base + PANEL:, :] - update[base + PANEL:, :]
        work_ref[:, base:base + PANEL, :] = panel * live_ref[...]
    start = pl.multiple_of(column_ref[0] * out_ref.shape[1], out_ref.shape[1])
    out_ref[...] = work_ref[:, pl.ds(start, out_ref.shape[1]), :]


def cholesky_upper(column_index, whole_rows, live, slab_width):
    blocks, samples, order = whole_rows.shape
    return pl.pallas_call(
        cholesky_kernel,
        out_shape=jax.ShapeDtypeStruct((blocks, slab_width, order), jnp.float32),
        grid_spec=pltpu.PrefetchScalarGridSpec(
            num_scalar_prefetch=1,
            grid=(1,),
            in_specs=[pl.BlockSpec(memory_space=pltpu.VMEM)] * 2,
            out_specs=pl.BlockSpec(memory_space=pltpu.VMEM),
            scratch_shapes=[pltpu.VMEM((blocks, order, order), jnp.float32)],
        ),
    )(column_index, whole_rows, live)


def local_mix_kernel(matrix_ref, signs_ref, table_ref, out_ref):
    slab_width = matrix_ref.shape[0]
    rows = out_ref.shape[1]
    groups = table_ref.shape[1] // rows

    def body(blk, carry):
        start = pl.multiple_of(blk * HB, HB)
        flips = (1 - 2 * signs_ref[:, pl.ds(start, HB)]).astype(jnp.float32)
        flipped = (matrix_ref[:, pl.ds(start, HB)].astype(jnp.float32) * flips).astype(jnp.bfloat16)
        for parity in range(2):
            mixed = lax.dot_general(
                table_ref[parity], flipped, (((1,), (1,)), ((), ())),
                preferred_element_type=jnp.float32,
            )
            for h in range(groups):
                out_ref[blk * groups + h, :, parity * slab_width:(parity + 1) * slab_width] = (
                    mixed[h * rows:(h + 1) * rows, :]
                )
        return carry

    lax.fori_loop(0, matrix_ref.shape[1] // HB, body, 0, unroll=True)


def local_mix(matrix, signs, table, row_devices):
    slab_width, shard_rows = matrix.shape
    sub_rows = shard_rows // row_devices
    return pl.pallas_call(
        local_mix_kernel,
        out_shape=jax.ShapeDtypeStruct((row_devices, sub_rows // 2, 2 * slab_width), jnp.float32),
        in_specs=[pl.BlockSpec(memory_space=pltpu.VMEM)] * 3,
        out_specs=pl.BlockSpec(memory_space=pltpu.VMEM),
    )(matrix, signs, table)


def walsh_sign_matrix(order):
    index_row = np.arange(order)
    parity = np.zeros((order, order), np.int64)
    for bit_place in range(order.bit_length() - 1):
        both = np.bitwise_and(index_row[:, None], index_row[None, :])
        parity = parity + np.bitwise_and(np.right_shift(both, bit_place), 1)
    return (1 - 2 * (parity % 2)).astype(np.float32)


def per_device(matrix, signs, samples, owners):
    slab_width = matrix.shape[0]
    shard_rows = matrix.shape[1]
    row_devices = lax.axis_size("rows")
    processor_number = lax.axis_index("rows")
    sub_rows = shard_rows // row_devices
    scale = 1.0 / math.sqrt(HB * row_devices)
    table = (walsh_sign_matrix(HB) * scale).reshape(HB // 2, 2, HB).transpose(1, 0, 2)
    outgoing = local_mix(matrix, signs.reshape(1, shard_rows), jnp.asarray(table, jnp.bfloat16), row_devices)
    received = lax.all_to_all(outgoing, "rows", split_axis=0, concat_axis=0, tiled=True)
    across = jnp.asarray(walsh_sign_matrix(row_devices))
    mixed = jnp.einsum(
        "st,tvl->svl", across, received, precision=lax.Precision.HIGHEST
    ).reshape(row_devices * sub_rows // 2, 2 * slab_width)

    block_total = samples.shape[0]
    block_ids = jnp.arange(block_total, dtype=jnp.int32)
    first_q = jnp.mod(processor_number - block_ids, row_devices)
    picks = jnp.stack([first_q, first_q + row_devices], axis=1)
    sample_values = jnp.take_along_axis(samples, picks, axis=1)
    shard_of = picks // (samples.shape[1] // row_devices)
    offsets = sample_values - shard_of * shard_rows - processor_number * sub_rows
    both_halves = jnp.take(mixed, shard_of * (sub_rows // 2) + offsets // 2, axis=0)
    chosen = jnp.where(
        (offsets % 2 == 1)[:, :, None], both_halves[:, :, slab_width:], both_halves[:, :, :slab_width]
    )

    owner_list = owners[:, 0]
    preceding_rows = jnp.logical_and(
        owner_list[None, :] == owner_list[:, None], block_ids[None, :] < block_ids[:, None]
    )
    ranks = jnp.sum(preceding_rows.astype(jnp.int32), axis=1)
    slots = owner_list * CAPB + ranks
    placing = (jnp.arange(row_devices * CAPB, dtype=jnp.int32)[:, None] == slots[None, :]).astype(
        jnp.float32
    )
    bundled = jnp.einsum("kb,bps->kps", placing, chosen, precision=lax.Precision.HIGHEST)
    bundled = bundled.reshape(row_devices, CAPB, 2 * slab_width)
    arriving = lax.all_to_all(bundled, "rows", split_axis=0, concat_axis=0, tiled=True)
    received_rows = jnp.transpose(arriving, (1, 0, 2)).reshape(CAPB, row_devices * 2, slab_width)
    whole_rows = lax.all_gather(received_rows, "cols", axis=2, tiled=True)
    owned_total = jnp.sum((owner_list == processor_number).astype(jnp.int32))
    live = (jnp.arange(CAPB, dtype=jnp.int32) < owned_total).astype(jnp.float32)
    live = jnp.broadcast_to(live[:, None, None], (CAPB, 1, whole_rows.shape[2]))
    column_index = lax.axis_index("cols").astype(jnp.int32).reshape(1)
    return cholesky_upper(column_index, whole_rows, live, slab_width)


def solution(mesh):
    in_specs = (P("cols", "rows"), P("rows"), P(), P())
    out_specs = P("rows", "cols", None)
    return jax.shard_map(
        per_device, mesh=mesh, in_specs=in_specs, out_specs=out_specs, check_vma=False
    )
```

```python
import math

import jax
import numpy as np
import jax.numpy as jnp
from jax import lax
from jax.experimental import pallas as pl
from jax.experimental.pallas import tpu as pltpu
from jax.sharding import PartitionSpec as P

HB = 128
SKETCH_ROW_COUNT = 256
CAPB = 4

PANEL = 32
STEP = 8


def cholesky_kernel(column_ref, rows_ref, live_ref, out_ref, work_ref):
    blocks, samples, order = rows_ref.shape
    for b in range(blocks):
        gram = lax.dot_general(
            rows_ref[b], rows_ref[b], (((0,), (0,)), ((), ())),
            precision=lax.Precision.HIGHEST, preferred_element_type=jnp.float32,
        ) / samples
        diagonal = (
            lax.broadcasted_iota(jnp.int32, (order, order), 0)
            == lax.broadcasted_iota(jnp.int32, (order, order), 1)
        )
        identity = jnp.where(diagonal, 1.0, 0.0)
        work_ref[b] = jnp.where(live_ref[b] > 0.0, gram, identity)
    lane = lax.broadcasted_iota(jnp.int32, (blocks, 1, order), 2)
    sub_panel = lax.broadcasted_iota(jnp.int32, (blocks, PANEL, order), 1)
    for p in range(order // PANEL):
        base = p * PANEL
        panel = work_ref[:, base:base + PANEL, :]
        for first in range(0, PANEL, STEP):
            columns = [
                jnp.broadcast_to(panel[:, :, base + first + m:base + first + m + 1], panel.shape)
                for m in range(STEP)
            ]
            factor_rows, factor_columns = [], []
            for m in range(STEP):
                jj = first + m
                column = columns[m]
                row = panel[:, jj:jj + 1, :]
                for earlier in range(m):
                    coupling = factor_columns[earlier][:, jj:jj + 1, :]
                    column = column - factor_columns[earlier] * coupling
                    row = row - coupling * factor_rows[earlier]
                inverse_root = lax.rsqrt(column[:, jj:jj + 1, :])
                factor_rows.append(jnp.where(lane >= base + jj, row * inverse_root, 0.0))
                factor_columns.append(jnp.where(sub_panel > jj, column * inverse_root, 0.0))
            for m in range(STEP):
                panel = panel - factor_columns[m] * factor_rows[m]
            for m in range(STEP):
                panel = jnp.where(sub_panel == first + m, factor_rows[m], panel)
        if p + 1 < order // PANEL:
            for b in range(blocks):
                update = lax.dot_general(
                    panel[b], panel[b], (((0,), (0,)), ((), ())),
                    precision=lax.Precision.HIGHEST, preferred_element_type=jnp.float32,
                )
                work_ref[b, base + PANEL:, :] = work_ref[b, base + PANEL:, :] - update[base + PANEL:, :]
        work_ref[:, base:base + PANEL, :] = panel * live_ref[...]
    start = pl.multiple_of(column_ref[0] * out_ref.shape[1], out_ref.shape[1])
    out_ref[...] = work_ref[:, pl.ds(start, out_ref.shape[1]), :]


def cholesky_upper(column_index, whole_rows, live, slab_width):
    blocks, samples, order = whole_rows.shape
    return pl.pallas_call(
        cholesky_kernel,
        out_shape=jax.ShapeDtypeStruct((blocks, slab_width, order), jnp.float32),
        grid_spec=pltpu.PrefetchScalarGridSpec(
            num_scalar_prefetch=1,
            grid=(1,),
            in_specs=[pl.BlockSpec(memory_space=pltpu.VMEM)] * 2,
            out_specs=pl.BlockSpec(memory_space=pltpu.VMEM),
            scratch_shapes=[pltpu.VMEM((blocks, order, order), jnp.float32)],
        ),
    )(column_index, whole_rows, live)


def local_mix_kernel(matrix_ref, signs_ref, table_ref, out_ref):
    slab_width = matrix_ref.shape[0]
    rows = out_ref.shape[1]
    groups = table_ref.shape[1] // rows

    def body(blk, carry):
        start = pl.multiple_of(blk * HB, HB)
        flips = (1 - 2 * signs_ref[:, pl.ds(start, HB)]).astype(jnp.float32)
        flipped = (matrix_ref[:, pl.ds(start, HB)].astype(jnp.float32) * flips).astype(jnp.bfloat16)
        for parity in range(2):
            mixed = lax.dot_general(
                table_ref[parity], flipped, (((1,), (1,)), ((), ())),
                preferred_element_type=jnp.float32,
            )
            for h in range(groups):
                out_ref[blk * groups + h, :, parity * slab_width:(parity + 1) * slab_width] = (
                    mixed[h * rows:(h + 1) * rows, :]
                )
        return carry

    lax.fori_loop(0, matrix_ref.shape[1] // HB, body, 0, unroll=True)


def local_mix(matrix, signs, table, row_devices):
    slab_width, shard_rows = matrix.shape
    sub_rows = shard_rows // row_devices
    return pl.pallas_call(
        local_mix_kernel,
        out_shape=jax.ShapeDtypeStruct((row_devices, sub_rows // 2, 2 * slab_width), jnp.float32),
        in_specs=[pl.BlockSpec(memory_space=pltpu.VMEM)] * 3,
        out_specs=pl.BlockSpec(memory_space=pltpu.VMEM),
    )(matrix, signs, table)


def walsh_sign_matrix(order):
    index_row = np.arange(order)
    parity = np.zeros((order, order), np.int64)
    for bit_place in range(order.bit_length() - 1):
        both = np.bitwise_and(index_row[:, None], index_row[None, :])
        parity = parity + np.bitwise_and(np.right_shift(both, bit_place), 1)
    return (1 - 2 * (parity % 2)).astype(np.float32)


def per_device(matrix, signs, samples, owners):
    slab_width = matrix.shape[0]
    shard_rows = matrix.shape[1]
    row_devices = lax.axis_size("rows")
    processor_number = lax.axis_index("rows")
    sub_rows = shard_rows // row_devices
    scale = 1.0 / math.sqrt(HB * row_devices)
    table = (walsh_sign_matrix(HB) * scale).reshape(HB // 2, 2, HB).transpose(1, 0, 2)
    outgoing = local_mix(matrix, signs.reshape(1, shard_rows), jnp.asarray(table, jnp.bfloat16), row_devices)
    received = lax.all_to_all(outgoing, "rows", split_axis=0, concat_axis=0, tiled=True)
    across = jnp.asarray(walsh_sign_matrix(row_devices))
    mixed = jnp.einsum(
        "st,tvl->svl", across, received, precision=lax.Precision.HIGHEST
    ).reshape(row_devices * sub_rows // 2, 2 * slab_width)

    block_total = samples.shape[0]
    block_ids = jnp.arange(block_total, dtype=jnp.int32)
    first_q = jnp.mod(processor_number - block_ids, row_devices)
    picks = jnp.stack([first_q, first_q + row_devices], axis=1)
    sample_values = jnp.take_along_axis(samples, picks, axis=1)
    shard_of = picks // (samples.shape[1] // row_devices)
    offsets = sample_values - shard_of * shard_rows - processor_number * sub_rows
    both_halves = jnp.take(mixed, shard_of * (sub_rows // 2) + offsets // 2, axis=0)
    chosen = jnp.where(
        (offsets % 2 == 1)[:, :, None], both_halves[:, :, slab_width:], both_halves[:, :, :slab_width]
    )

    owner_list = owners[:, 0]
    preceding_rows = jnp.logical_and(
        owner_list[None, :] == owner_list[:, None], block_ids[None, :] < block_ids[:, None]
    )
    ranks = jnp.sum(preceding_rows.astype(jnp.int32), axis=1)
    slots = owner_list * CAPB + ranks
    placing = (jnp.arange(row_devices * CAPB, dtype=jnp.int32)[:, None] == slots[None, :]).astype(
        jnp.float32
    )
    bundled = jnp.einsum("kb,bps->kps", placing, chosen, precision=lax.Precision.HIGHEST)
    bundled = bundled.reshape(row_devices, CAPB, 2 * slab_width)
    arriving = lax.all_to_all(bundled, "rows", split_axis=0, concat_axis=0, tiled=True)
    received_rows = jnp.transpose(arriving, (1, 0, 2)).reshape(CAPB, row_devices * 2, slab_width)
    whole_rows = lax.all_gather(received_rows, "cols", axis=2, tiled=True)
    owned_total = jnp.sum((owner_list == processor_number).astype(jnp.int32))
    live = (jnp.arange(CAPB, dtype=jnp.int32) < owned_total).astype(jnp.float32)
    live = jnp.broadcast_to(live[:, None, None], (CAPB, 1, whole_rows.shape[2]))
    column_index = lax.axis_index("cols").astype(jnp.int32).reshape(1)
    return cholesky_upper(column_index, whole_rows, live, slab_width)


def solution(mesh):
    in_specs = (P("cols", "rows"), P("rows"), P(), P())
    out_specs = P("rows", "cols", None)
    return jax.shard_map(
        per_device, mesh=mesh, in_specs=in_specs, out_specs=out_specs, check_vma=False
    )
```

```python
import math

import jax
import numpy as np
import jax.numpy as jnp
from jax import lax
from jax.experimental import pallas as pl
from jax.experimental.pallas import tpu as pltpu
from jax.sharding import PartitionSpec as P

HB = 128
SKETCH_ROW_COUNT = 256
CAPB = 4

PANEL = 32
STEP = 8


def cholesky_kernel(scalar_ref, rows_ref, out_ref, work_ref):
    blocks, samples, order = rows_ref.shape
    for b in range(blocks):
        gram = lax.dot_general(
            rows_ref[b], rows_ref[b], (((0,), (0,)), ((), ())),
            precision=lax.Precision.HIGHEST, preferred_element_type=jnp.float32,
        ) / samples
        diagonal = (
            lax.broadcasted_iota(jnp.int32, (order, order), 0)
            == lax.broadcasted_iota(jnp.int32, (order, order), 1)
        )
        identity = jnp.where(diagonal, 1.0, 0.0)
        work_ref[b] = jnp.where(b < scalar_ref[1], gram, identity)
    lane = lax.broadcasted_iota(jnp.int32, (blocks, 1, order), 2)
    sub_panel = lax.broadcasted_iota(jnp.int32, (blocks, PANEL, order), 1)
    for p in range(order // PANEL):
        base = p * PANEL
        panel = work_ref[:, base:base + PANEL, :]
        for first in range(0, PANEL, STEP):
            columns = [
                jnp.broadcast_to(panel[:, :, base + first + m:base + first + m + 1], panel.shape)
                for m in range(STEP)
            ]
            factor_rows, factor_columns = [], []
            for m in range(STEP):
                jj = first + m
                column = columns[m]
                row = panel[:, jj:jj + 1, :]
                for earlier in range(m):
                    coupling = factor_columns[earlier][:, jj:jj + 1, :]
                    column = column - factor_columns[earlier] * coupling
                    row = row - coupling * factor_rows[earlier]
                inverse_root = lax.rsqrt(column[:, jj:jj + 1, :])
                factor_rows.append(jnp.where(lane >= base + jj, row * inverse_root, 0.0))
                factor_columns.append(jnp.where(sub_panel > jj, column * inverse_root, 0.0))
            for m in range(STEP):
                panel = panel - factor_columns[m] * factor_rows[m]
            for m in range(STEP):
                panel = jnp.where(sub_panel == first + m, factor_rows[m], panel)
        if p + 1 < order // PANEL:
            for b in range(blocks):
                update = lax.dot_general(
                    panel[b], panel[b], (((0,), (0,)), ((), ())),
                    precision=lax.Precision.HIGHEST, preferred_element_type=jnp.float32,
                )
                work_ref[b, base + PANEL:, :] = work_ref[b, base + PANEL:, :] - update[base + PANEL:, :]
        work_ref[:, base:base + PANEL, :] = panel
    start = pl.multiple_of(scalar_ref[0] * out_ref.shape[1], out_ref.shape[1])
    for b in range(blocks):
        out_ref[b] = jnp.where(b < scalar_ref[1], work_ref[b, pl.ds(start, out_ref.shape[1]), :], 0.0)


def cholesky_upper(scalars, whole_rows, slab_width):
    blocks, samples, order = whole_rows.shape
    return pl.pallas_call(
        cholesky_kernel,
        out_shape=jax.ShapeDtypeStruct((blocks, slab_width, order), jnp.float32),
        grid_spec=pltpu.PrefetchScalarGridSpec(
            num_scalar_prefetch=1,
            grid=(1,),
            in_specs=[pl.BlockSpec(memory_space=pltpu.VMEM)],
            out_specs=pl.BlockSpec(memory_space=pltpu.VMEM),
            scratch_shapes=[pltpu.VMEM((blocks, order, order), jnp.float32)],
        ),
    )(scalars, whole_rows)


def local_mix_kernel(matrix_ref, signs_ref, table_ref, out_ref):
    slab_width = matrix_ref.shape[0]
    rows = out_ref.shape[1]
    groups = table_ref.shape[1] // rows

    def body(blk, carry):
        start = pl.multiple_of(blk * HB, HB)
        flips = (1 - 2 * signs_ref[:, pl.ds(start, HB)]).astype(jnp.float32)
        flipped = (matrix_ref[:, pl.ds(start, HB)].astype(jnp.float32) * flips).astype(jnp.bfloat16)
        for parity in range(2):
            mixed = lax.dot_general(
                table_ref[parity], flipped, (((1,), (1,)), ((), ())),
                preferred_element_type=jnp.float32,
            )
            for h in range(groups):
                out_ref[blk * groups + h, :, parity * slab_width:(parity + 1) * slab_width] = (
                    mixed[h * rows:(h + 1) * rows, :]
                )
        return carry

    lax.fori_loop(0, matrix_ref.shape[1] // HB, body, 0, unroll=True)


def local_mix(matrix, signs, table, row_devices):
    slab_width, shard_rows = matrix.shape
    sub_rows = shard_rows // row_devices
    return pl.pallas_call(
        local_mix_kernel,
        out_shape=jax.ShapeDtypeStruct((row_devices, sub_rows // 2, 2 * slab_width), jnp.float32),
        in_specs=[pl.BlockSpec(memory_space=pltpu.VMEM)] * 3,
        out_specs=pl.BlockSpec(memory_space=pltpu.VMEM),
    )(matrix, signs, table)


def walsh_sign_matrix(order):
    index_row = np.arange(order)
    parity = np.zeros((order, order), np.int64)
    for bit_place in range(order.bit_length() - 1):
        both = np.bitwise_and(index_row[:, None], index_row[None, :])
        parity = parity + np.bitwise_and(np.right_shift(both, bit_place), 1)
    return (1 - 2 * (parity % 2)).astype(np.float32)


def per_device(matrix, signs, samples, owners):
    slab_width = matrix.shape[0]
    shard_rows = matrix.shape[1]
    row_devices = lax.axis_size("rows")
    processor_number = lax.axis_index("rows")
    sub_rows = shard_rows // row_devices
    scale = 1.0 / math.sqrt(HB * row_devices)
    table = (walsh_sign_matrix(HB) * scale).reshape(HB // 2, 2, HB).transpose(1, 0, 2)
    outgoing = local_mix(matrix, signs.reshape(1, shard_rows), jnp.asarray(table, jnp.bfloat16), row_devices)
    received = lax.all_to_all(outgoing, "rows", split_axis=0, concat_axis=0, tiled=True)
    across = jnp.asarray(walsh_sign_matrix(row_devices))
    mixed = jnp.einsum(
        "st,tvl->svl", across, received, precision=lax.Precision.HIGHEST
    ).reshape(row_devices * sub_rows // 2, 2 * slab_width)

    block_total = samples.shape[0]
    block_ids = jnp.arange(block_total, dtype=jnp.int32)
    first_q = jnp.mod(processor_number - block_ids, row_devices)
    picks = jnp.stack([first_q, first_q + row_devices], axis=1)
    sample_values = jnp.take_along_axis(samples, picks, axis=1)
    shard_of = picks // (samples.shape[1] // row_devices)
    offsets = sample_values - shard_of * shard_rows - processor_number * sub_rows
    both_halves = jnp.take(mixed, shard_of * (sub_rows // 2) + offsets // 2, axis=0)
    chosen = jnp.where(
        (offsets % 2 == 1)[:, :, None], both_halves[:, :, slab_width:], both_halves[:, :, :slab_width]
    )

    owner_list = owners[:, 0]
    preceding_rows = jnp.logical_and(
        owner_list[None, :] == owner_list[:, None], block_ids[None, :] < block_ids[:, None]
    )
    ranks = jnp.sum(preceding_rows.astype(jnp.int32), axis=1)
    slots = owner_list * CAPB + ranks
    placing = (jnp.arange(row_devices * CAPB, dtype=jnp.int32)[:, None] == slots[None, :]).astype(
        jnp.float32
    )
    bundled = jnp.einsum("kb,bps->kps", placing, chosen, precision=lax.Precision.HIGHEST)
    bundled = bundled.reshape(row_devices, CAPB, 2 * slab_width)
    arriving = lax.all_to_all(bundled, "rows", split_axis=0, concat_axis=0, tiled=True)
    received_rows = jnp.transpose(arriving, (1, 0, 2)).reshape(CAPB, row_devices * 2, slab_width)
    whole_rows = lax.all_gather(received_rows, "cols", axis=2, tiled=True)
    owned_total = jnp.sum((owner_list == processor_number).astype(jnp.int32))
    scalars = jnp.stack([lax.axis_index("cols").astype(jnp.int32), owned_total.astype(jnp.int32)])
    return cholesky_upper(scalars, whole_rows, slab_width)


def solution(mesh):
    in_specs = (P("cols", "rows"), P("rows"), P(), P())
    out_specs = P("rows", "cols", None)
    return jax.shard_map(
        per_device, mesh=mesh, in_specs=in_specs, out_specs=out_specs, check_vma=False
    )
```

```python
import math

import jax
import numpy as np
import jax.numpy as jnp
from jax import lax
from jax.experimental import pallas as pl
from jax.experimental.pallas import tpu as pltpu
from jax.sharding import PartitionSpec as P

HB = 128
SKETCH_ROW_COUNT = 256
CAPB = 4

PANEL = 32
STEP = 8


def cholesky_kernel(scalar_ref, rows_ref, out_ref, work_ref):
    blocks, samples, order = rows_ref.shape
    for b in range(blocks):
        gram = lax.dot_general(
            rows_ref[b], rows_ref[b], (((0,), (0,)), ((), ())),
            precision=lax.Precision.HIGHEST, preferred_element_type=jnp.float32,
        ) / samples
        diagonal = (
            lax.broadcasted_iota(jnp.int32, (order, order), 0)
            == lax.broadcasted_iota(jnp.int32, (order, order), 1)
        )
        identity = jnp.where(diagonal, 1.0, 0.0)
        work_ref[b] = jnp.where(b < scalar_ref[1], gram, identity)
    lane = lax.broadcasted_iota(jnp.int32, (blocks, 1, order), 2)
    sub_panel = lax.broadcasted_iota(jnp.int32, (blocks, PANEL, order), 1)
    for p in range(order // PANEL):
        base = p * PANEL
        panel = work_ref[:, base:base + PANEL, :]
        for first in range(0, PANEL, STEP):
            columns = [
                jnp.broadcast_to(panel[:, :, base + first + m:base + first + m + 1], panel.shape)
                for m in range(STEP)
            ]
            factor_rows, factor_columns = [], []
            for m in range(STEP):
                jj = first + m
                column = columns[m]
                row = panel[:, jj:jj + 1, :]
                for earlier in range(m):
                    coupling = factor_columns[earlier][:, jj:jj + 1, :]
                    column = column - factor_columns[earlier] * coupling
                    row = row - coupling * factor_rows[earlier]
                inverse_root = lax.rsqrt(column[:, jj:jj + 1, :])
                factor_rows.append(jnp.where(lane >= base + jj, row * inverse_root, 0.0))
                factor_columns.append(jnp.where(sub_panel > jj, column * inverse_root, 0.0))
            for m in range(STEP):
                panel = panel - factor_columns[m] * factor_rows[m]
            for m in range(STEP):
                panel = jnp.where(sub_panel == first + m, factor_rows[m], panel)
        if p + 1 < order // PANEL:
            for b in range(blocks):
                update = lax.dot_general(
                    panel[b], panel[b], (((0,), (0,)), ((), ())),
                    precision=lax.Precision.HIGHEST, preferred_element_type=jnp.float32,
                )
                work_ref[b, base + PANEL:, :] = work_ref[b, base + PANEL:, :] - update[base + PANEL:, :]
        work_ref[:, base:base + PANEL, :] = panel
    start = pl.multiple_of(scalar_ref[0] * out_ref.shape[1], out_ref.shape[1])
    for b in range(blocks):
        out_ref[b] = jnp.where(b < scalar_ref[1], work_ref[b, pl.ds(start, out_ref.shape[1]), :], 0.0)


def cholesky_upper(scalars, whole_rows, slab_width):
    blocks, samples, order = whole_rows.shape
    return pl.pallas_call(
        cholesky_kernel,
        out_shape=jax.ShapeDtypeStruct((blocks, slab_width, order), jnp.float32),
        grid_spec=pltpu.PrefetchScalarGridSpec(
            num_scalar_prefetch=1,
            grid=(1,),
            in_specs=[pl.BlockSpec(memory_space=pltpu.VMEM)],
            out_specs=pl.BlockSpec(memory_space=pltpu.VMEM),
            scratch_shapes=[pltpu.VMEM((blocks, order, order), jnp.float32)],
        ),
    )(scalars, whole_rows)


def local_mix_kernel(matrix_ref, signs_ref, table_ref, out_ref):
    slab_width = matrix_ref.shape[0]
    rows = out_ref.shape[1]
    groups = table_ref.shape[1] // rows

    def body(blk, carry):
        start = pl.multiple_of(blk * HB, HB)
        flips = (1 - 2 * signs_ref[:, pl.ds(start, HB)]).astype(jnp.float32)
        flipped = (matrix_ref[:, pl.ds(start, HB)].astype(jnp.float32) * flips).astype(jnp.bfloat16)
        for parity in range(2):
            mixed = lax.dot_general(
                table_ref[parity], flipped, (((1,), (1,)), ((), ())),
                preferred_element_type=jnp.float32,
            )
            for h in range(groups):
                out_ref[blk * groups + h, :, parity * slab_width:(parity + 1) * slab_width] = (
                    mixed[h * rows:(h + 1) * rows, :]
                )
        return carry

    lax.fori_loop(0, matrix_ref.shape[1] // HB, body, 0, unroll=True)


def local_mix(matrix, signs, table, row_devices):
    slab_width, shard_rows = matrix.shape
    sub_rows = shard_rows // row_devices
    return pl.pallas_call(
        local_mix_kernel,
        out_shape=jax.ShapeDtypeStruct((row_devices, sub_rows // 2, 2 * slab_width), jnp.float32),
        in_specs=[pl.BlockSpec(memory_space=pltpu.VMEM)] * 3,
        out_specs=pl.BlockSpec(memory_space=pltpu.VMEM),
    )(matrix, signs, table)


def walsh_sign_matrix(order):
    index_row = np.arange(order)
    parity = np.zeros((order, order), np.int64)
    for bit_place in range(order.bit_length() - 1):
        both = np.bitwise_and(index_row[:, None], index_row[None, :])
        parity = parity + np.bitwise_and(np.right_shift(both, bit_place), 1)
    return (1 - 2 * (parity % 2)).astype(np.float32)


def per_device(matrix, signs, samples, owners):
    slab_width = matrix.shape[0]
    shard_rows = matrix.shape[1]
    row_devices = lax.axis_size("rows")
    processor_number = lax.axis_index("rows")
    sub_rows = shard_rows // row_devices
    scale = 1.0 / math.sqrt(HB * row_devices)
    table = (walsh_sign_matrix(HB) * scale).reshape(HB // 2, 2, HB).transpose(1, 0, 2)
    outgoing = local_mix(matrix, signs.reshape(1, shard_rows), jnp.asarray(table, jnp.bfloat16), row_devices)
    received = lax.all_to_all(outgoing, "rows", split_axis=0, concat_axis=0, tiled=True)
    block_total = samples.shape[0]
    block_ids = jnp.arange(block_total, dtype=jnp.int32)
    owner_list = owners[:, 0]
    preceding_rows = jnp.logical_and(
        owner_list[None, :] == owner_list[:, None], block_ids[None, :] < block_ids[:, None]
    )
    ranks = jnp.sum(preceding_rows.astype(jnp.int32), axis=1)
    slots = owner_list * CAPB + ranks
    slot_ids = jnp.arange(row_devices * CAPB, dtype=jnp.int32)
    match = slots[None, :] == slot_ids[:, None]
    filled = jnp.any(match, axis=1)

    first_q = jnp.mod(processor_number - block_ids, row_devices)
    sample_pos = jnp.arange(samples.shape[1], dtype=jnp.int32)
    per_shard = samples.shape[1] // row_devices
    row_parts, parity_parts = [], []
    for half in range(per_shard):
        q = first_q + half * row_devices
        value = jnp.sum(jnp.where(sample_pos[None, :] == q[:, None], samples, 0), axis=1)
        shard = q // per_shard
        offset = value - shard * shard_rows - processor_number * sub_rows
        row = jnp.sum(jnp.where(match, (shard * (sub_rows // 2) + offset // 2)[None, :], 0), axis=1)
        parity = jnp.sum(jnp.where(match, (offset % 2)[None, :], 0), axis=1)
        row_parts.append(row)
        parity_parts.append(parity)
    slot_rows = jnp.stack(row_parts, axis=1)
    slot_parity = jnp.stack(parity_parts, axis=1)

    across = jnp.asarray(walsh_sign_matrix(row_devices))
    mixed = jnp.einsum(
        "st,tvl->svl", across, received, precision=lax.Precision.HIGHEST
    ).reshape(row_devices * sub_rows // 2, 2 * slab_width)
    both_halves = jnp.take(mixed, slot_rows, axis=0)
    chosen = jnp.where(
        (slot_parity == 1)[:, :, None], both_halves[:, :, slab_width:], both_halves[:, :, :slab_width]
    )
    bundled = jnp.where(filled[:, None, None], chosen, 0.0).reshape(row_devices, CAPB, per_shard * slab_width)
    arriving = lax.all_to_all(bundled, "rows", split_axis=0, concat_axis=0, tiled=True)
    received_rows = jnp.transpose(arriving, (1, 0, 2)).reshape(CAPB, row_devices * 2, slab_width)
    whole_rows = lax.all_gather(received_rows, "cols", axis=2, tiled=True)
    owned_total = jnp.sum((owner_list == processor_number).astype(jnp.int32))
    scalars = jnp.stack([lax.axis_index("cols").astype(jnp.int32), owned_total.astype(jnp.int32)])
    return cholesky_upper(scalars, whole_rows, slab_width)


def solution(mesh):
    in_specs = (P("cols", "rows"), P("rows"), P(), P())
    out_specs = P("rows", "cols", None)
    return jax.shard_map(
        per_device, mesh=mesh, in_specs=in_specs, out_specs=out_specs, check_vma=False
    )
```

```python
import math

import jax
import numpy as np
import jax.numpy as jnp
from jax import lax
from jax.experimental import pallas as pl
from jax.experimental.pallas import tpu as pltpu
from jax.sharding import PartitionSpec as P

HB = 128
SKETCH_ROW_COUNT = 256
CAPB = 4

PANEL = 32
SAMPLES_PER_SHARD = 2
STEP = 8


def cholesky_kernel(scalar_ref, rows_ref, out_ref, work_ref):
    cores, blocks, sources, lanes = rows_ref.shape
    width = lanes // SAMPLES_PER_SHARD
    order = cores * width
    samples = sources * SAMPLES_PER_SHARD
    diagonal = (
        lax.broadcasted_iota(jnp.int32, (width, width), 0)
        == lax.broadcasted_iota(jnp.int32, (width, width), 1)
    )
    for b in range(blocks):
        for left in range(cores):
            for right in range(cores):
                product = None
                for j in range(SAMPLES_PER_SHARD):
                    term = lax.dot_general(
                        rows_ref[left, b, :, j * width:(j + 1) * width],
                        rows_ref[right, b, :, j * width:(j + 1) * width],
                        (((0,), (0,)), ((), ())),
                        precision=lax.Precision.HIGHEST, preferred_element_type=jnp.float32,
                    )
                    product = term if product is None else product + term
                fill = jnp.where(diagonal, 1.0, 0.0) if left == right else jnp.zeros((width, width), jnp.float32)
                work_ref[b, left * width:(left + 1) * width, right * width:(right + 1) * width] = jnp.where(
                    b < scalar_ref[1], product / samples, fill
                )
    lane = lax.broadcasted_iota(jnp.int32, (blocks, 1, order), 2)
    sub_panel = lax.broadcasted_iota(jnp.int32, (blocks, PANEL, order), 1)
    for p in range(order // PANEL):
        base = p * PANEL
        panel = work_ref[:, base:base + PANEL, :]
        for first in range(0, PANEL, STEP):
            columns = [
                jnp.broadcast_to(panel[:, :, base + first + m:base + first + m + 1], panel.shape)
                for m in range(STEP)
            ]
            factor_rows, factor_columns = [], []
            for m in range(STEP):
                jj = first + m
                column = columns[m]
                row = panel[:, jj:jj + 1, :]
                for earlier in range(m):
                    coupling = factor_columns[earlier][:, jj:jj + 1, :]
                    column = column - factor_columns[earlier] * coupling
                    row = row - coupling * factor_rows[earlier]
                inverse_root = lax.rsqrt(column[:, jj:jj + 1, :])
                factor_rows.append(jnp.where(lane >= base + jj, row * inverse_root, 0.0))
                factor_columns.append(jnp.where(sub_panel > jj, column * inverse_root, 0.0))
            for m in range(STEP):
                panel = panel - factor_columns[m] * factor_rows[m]
            for m in range(STEP):
                panel = jnp.where(sub_panel == first + m, factor_rows[m], panel)
        if p + 1 < order // PANEL:
            for b in range(blocks):
                update = lax.dot_general(
                    panel[b], panel[b], (((0,), (0,)), ((), ())),
                    precision=lax.Precision.HIGHEST, preferred_element_type=jnp.float32,
                )
                work_ref[b, base + PANEL:, :] = work_ref[b, base + PANEL:, :] - update[base + PANEL:, :]
        work_ref[:, base:base + PANEL, :] = panel
    start = pl.multiple_of(scalar_ref[0] * out_ref.shape[1], out_ref.shape[1])
    for b in range(blocks):
        out_ref[b] = jnp.where(b < scalar_ref[1], work_ref[b, pl.ds(start, out_ref.shape[1]), :], 0.0)


def cholesky_upper(scalars, whole_rows, slab_width):
    cores, blocks, _, lanes = whole_rows.shape
    order = cores * slab_width
    return pl.pallas_call(
        cholesky_kernel,
        out_shape=jax.ShapeDtypeStruct((blocks, slab_width, order), jnp.float32),
        grid_spec=pltpu.PrefetchScalarGridSpec(
            num_scalar_prefetch=1,
            grid=(1,),
            in_specs=[pl.BlockSpec(memory_space=pltpu.VMEM)],
            out_specs=pl.BlockSpec(memory_space=pltpu.VMEM),
            scratch_shapes=[pltpu.VMEM((blocks, order, order), jnp.float32)],
        ),
    )(scalars, whole_rows)


def local_mix_kernel(matrix_ref, signs_ref, table_ref, out_ref):
    slab_width = matrix_ref.shape[0]
    rows = out_ref.shape[1]
    groups = table_ref.shape[1] // rows

    def body(blk, carry):
        start = pl.multiple_of(blk * HB, HB)
        flips = (1 - 2 * signs_ref[:, pl.ds(start, HB)]).astype(jnp.float32)
        flipped = (matrix_ref[:, pl.ds(start, HB)].astype(jnp.float32) * flips).astype(jnp.bfloat16)
        for parity in range(2):
            mixed = lax.dot_general(
                table_ref[parity], flipped, (((1,), (1,)), ((), ())),
                preferred_element_type=jnp.float32,
            )
            for h in range(groups):
                out_ref[blk * groups + h, :, parity * slab_width:(parity + 1) * slab_width] = (
                    mixed[h * rows:(h + 1) * rows, :]
                )
        return carry

    lax.fori_loop(0, matrix_ref.shape[1] // HB, body, 0, unroll=True)


def local_mix(matrix, signs, table, row_devices):
    slab_width, shard_rows = matrix.shape
    sub_rows = shard_rows // row_devices
    return pl.pallas_call(
        local_mix_kernel,
        out_shape=jax.ShapeDtypeStruct((row_devices, sub_rows // 2, 2 * slab_width), jnp.float32),
        in_specs=[pl.BlockSpec(memory_space=pltpu.VMEM)] * 3,
        out_specs=pl.BlockSpec(memory_space=pltpu.VMEM),
    )(matrix, signs, table)


def walsh_sign_matrix(order):
    index_row = np.arange(order)
    parity = np.zeros((order, order), np.int64)
    for bit_place in range(order.bit_length() - 1):
        both = np.bitwise_and(index_row[:, None], index_row[None, :])
        parity = parity + np.bitwise_and(np.right_shift(both, bit_place), 1)
    return (1 - 2 * (parity % 2)).astype(np.float32)


def per_device(matrix, signs, samples, owners):
    slab_width = matrix.shape[0]
    shard_rows = matrix.shape[1]
    row_devices = lax.axis_size("rows")
    processor_number = lax.axis_index("rows")
    sub_rows = shard_rows // row_devices
    scale = 1.0 / math.sqrt(HB * row_devices)
    table = (walsh_sign_matrix(HB) * scale).reshape(HB // 2, 2, HB).transpose(1, 0, 2)
    outgoing = local_mix(matrix, signs.reshape(1, shard_rows), jnp.asarray(table, jnp.bfloat16), row_devices)
    received = lax.all_to_all(outgoing, "rows", split_axis=0, concat_axis=0, tiled=True)
    across = jnp.asarray(walsh_sign_matrix(row_devices))
    mixed = jnp.einsum(
        "st,tvl->svl", across, received, precision=lax.Precision.HIGHEST
    ).reshape(row_devices * sub_rows // 2, 2 * slab_width)

    block_total = samples.shape[0]
    block_ids = jnp.arange(block_total, dtype=jnp.int32)
    first_q = jnp.mod(processor_number - block_ids, row_devices)
    picks = jnp.stack([first_q, first_q + row_devices], axis=1)
    sample_values = jnp.take_along_axis(samples, picks, axis=1)
    shard_of = picks // (samples.shape[1] // row_devices)
    offsets = sample_values - shard_of * shard_rows - processor_number * sub_rows
    both_halves = jnp.take(mixed, shard_of * (sub_rows // 2) + offsets // 2, axis=0)
    chosen = jnp.where(
        (offsets % 2 == 1)[:, :, None], both_halves[:, :, slab_width:], both_halves[:, :, :slab_width]
    )

    owner_list = owners[:, 0]
    preceding_rows = jnp.logical_and(
        owner_list[None, :] == owner_list[:, None], block_ids[None, :] < block_ids[:, None]
    )
    ranks = jnp.sum(preceding_rows.astype(jnp.int32), axis=1)
    slots = owner_list * CAPB + ranks
    placing = (jnp.arange(row_devices * CAPB, dtype=jnp.int32)[:, None] == slots[None, :]).astype(
        jnp.float32
    )
    bundled = jnp.einsum("kb,bps->kps", placing, chosen, precision=lax.Precision.HIGHEST)
    bundled = bundled.reshape(row_devices, CAPB, 2 * slab_width).transpose(1, 0, 2)
    arriving = lax.all_to_all(bundled, "rows", split_axis=1, concat_axis=1, tiled=True)
    whole_rows = lax.all_gather(arriving, "cols", axis=0, tiled=False)
    owned_total = jnp.sum((owner_list == processor_number).astype(jnp.int32))
    scalars = jnp.stack([lax.axis_index("cols").astype(jnp.int32), owned_total.astype(jnp.int32)])
    return cholesky_upper(scalars, whole_rows, slab_width)


def solution(mesh):
    in_specs = (P("cols", "rows"), P("rows"), P(), P())
    out_specs = P("rows", "cols", None)
    return jax.shard_map(
        per_device, mesh=mesh, in_specs=in_specs, out_specs=out_specs, check_vma=False
    )
```

```python
import math

import jax
import numpy as np
import jax.numpy as jnp
from jax import lax
from jax.experimental import pallas as pl
from jax.experimental.pallas import tpu as pltpu
from jax.sharding import PartitionSpec as P

HB = 128
SKETCH_ROW_COUNT = 256
CAPB = 4

PANEL = 32
STEP = 8


def cholesky_kernel(scalar_ref, rows_ref, out_ref, work_ref):
    blocks, samples, order = rows_ref.shape
    for b in range(blocks):
        gram = lax.dot_general(
            rows_ref[b], rows_ref[b], (((0,), (0,)), ((), ())),
            precision=lax.Precision.HIGHEST, preferred_element_type=jnp.float32,
        ) / samples
        diagonal = (
            lax.broadcasted_iota(jnp.int32, (order, order), 0)
            == lax.broadcasted_iota(jnp.int32, (order, order), 1)
        )
        identity = jnp.where(diagonal, 1.0, 0.0)
        work_ref[b] = jnp.where(b < scalar_ref[1], gram, identity)
    lane = lax.broadcasted_iota(jnp.int32, (blocks, 1, order), 2)
    sub_panel = lax.broadcasted_iota(jnp.int32, (blocks, PANEL, order), 1)
    for p in range(order // PANEL):
        base = p * PANEL
        panel = work_ref[:, base:base + PANEL, :]
        for first in range(0, PANEL, STEP):
            columns = [
                jnp.broadcast_to(panel[:, :, base + first + m:base + first + m + 1], panel.shape)
                for m in range(STEP)
            ]
            factor_rows, factor_columns = [], []
            for m in range(STEP):
                jj = first + m
                column = columns[m]
                row = panel[:, jj:jj + 1, :]
                for earlier in range(m):
                    coupling = factor_columns[earlier][:, jj:jj + 1, :]
                    column = column - factor_columns[earlier] * coupling
                    row = row - coupling * factor_rows[earlier]
                inverse_root = lax.rsqrt(column[:, jj:jj + 1, :])
                factor_rows.append(jnp.where(lane >= base + jj, row * inverse_root, 0.0))
                factor_columns.append(jnp.where(sub_panel > jj, column * inverse_root, 0.0))
            for m in range(STEP):
                panel = panel - factor_columns[m] * factor_rows[m]
            for m in range(STEP):
                panel = jnp.where(sub_panel == first + m, factor_rows[m], panel)
        if p + 1 < order // PANEL:
            for b in range(blocks):
                update = lax.dot_general(
                    panel[b], panel[b], (((0,), (0,)), ((), ())),
                    precision=lax.Precision.HIGHEST, preferred_element_type=jnp.float32,
                )
                work_ref[b, base + PANEL:, :] = work_ref[b, base + PANEL:, :] - update[base + PANEL:, :]
        work_ref[:, base:base + PANEL, :] = panel
    start = pl.multiple_of(scalar_ref[0] * out_ref.shape[1], out_ref.shape[1])
    for b in range(blocks):
        out_ref[b] = jnp.where(b < scalar_ref[1], work_ref[b, pl.ds(start, out_ref.shape[1]), :], 0.0)


def cholesky_upper(scalars, whole_rows, slab_width):
    blocks, samples, order = whole_rows.shape
    return pl.pallas_call(
        cholesky_kernel,
        out_shape=jax.ShapeDtypeStruct((blocks, slab_width, order), jnp.float32),
        grid_spec=pltpu.PrefetchScalarGridSpec(
            num_scalar_prefetch=1,
            grid=(1,),
            in_specs=[pl.BlockSpec(memory_space=pltpu.VMEM)],
            out_specs=pl.BlockSpec(memory_space=pltpu.VMEM),
            scratch_shapes=[pltpu.VMEM((blocks, order, order), jnp.float32)],
        ),
    )(scalars, whole_rows)


def local_mix_kernel(matrix_ref, signs_ref, table_ref, out_ref):
    slab_width = matrix_ref.shape[0]
    rows = out_ref.shape[1]
    groups = table_ref.shape[1] // rows

    def body(blk, carry):
        start = pl.multiple_of(blk * HB, HB)
        flips = (1 - 2 * signs_ref[:, pl.ds(start, HB)]).astype(jnp.float32)
        flipped = (matrix_ref[:, pl.ds(start, HB)].astype(jnp.float32) * flips).astype(jnp.bfloat16)
        for parity in range(2):
            mixed = lax.dot_general(
                table_ref[parity], flipped, (((1,), (1,)), ((), ())),
                preferred_element_type=jnp.float32,
            )
            for h in range(groups):
                out_ref[blk * groups + h, :, parity * slab_width:(parity + 1) * slab_width] = (
                    mixed[h * rows:(h + 1) * rows, :]
                )
        return carry

    lax.fori_loop(0, matrix_ref.shape[1] // HB, body, 0, unroll=True)


def local_mix(matrix, signs, table, row_devices, steps=4):
    slab_width, shard_rows = matrix.shape
    sub_rows = shard_rows // row_devices
    span = shard_rows // steps
    return pl.pallas_call(
        local_mix_kernel,
        out_shape=jax.ShapeDtypeStruct((row_devices, sub_rows // 2, 2 * slab_width), jnp.float32),
        grid=(steps,),
        in_specs=[
            pl.BlockSpec((slab_width, span), lambda i: (0, i)),
            pl.BlockSpec((1, span), lambda i: (0, i)),
            pl.BlockSpec(table.shape, lambda i: (0, 0, 0)),
        ],
        out_specs=pl.BlockSpec((row_devices // steps, sub_rows // 2, 2 * slab_width), lambda i: (i, 0, 0)),
    )(matrix, signs, table)


def walsh_sign_matrix(order):
    index_row = np.arange(order)
    parity = np.zeros((order, order), np.int64)
    for bit_place in range(order.bit_length() - 1):
        both = np.bitwise_and(index_row[:, None], index_row[None, :])
        parity = parity + np.bitwise_and(np.right_shift(both, bit_place), 1)
    return (1 - 2 * (parity % 2)).astype(np.float32)


def per_device(matrix, signs, samples, owners):
    slab_width = matrix.shape[0]
    shard_rows = matrix.shape[1]
    row_devices = lax.axis_size("rows")
    processor_number = lax.axis_index("rows")
    sub_rows = shard_rows // row_devices
    scale = 1.0 / math.sqrt(HB * row_devices)
    table = (walsh_sign_matrix(HB) * scale).reshape(HB // 2, 2, HB).transpose(1, 0, 2)
    outgoing = local_mix(matrix, signs.reshape(1, shard_rows), jnp.asarray(table, jnp.bfloat16), row_devices)
    received = lax.all_to_all(outgoing, "rows", split_axis=0, concat_axis=0, tiled=True)
    across = jnp.asarray(walsh_sign_matrix(row_devices))
    mixed = jnp.einsum(
        "st,tvl->svl", across, received, precision=lax.Precision.HIGHEST
    ).reshape(row_devices * sub_rows // 2, 2 * slab_width)

    block_total = samples.shape[0]
    block_ids = jnp.arange(block_total, dtype=jnp.int32)
    first_q = jnp.mod(processor_number - block_ids, row_devices)
    picks = jnp.stack([first_q, first_q + row_devices], axis=1)
    sample_values = jnp.take_along_axis(samples, picks, axis=1)
    shard_of = picks // (samples.shape[1] // row_devices)
    offsets = sample_values - shard_of * shard_rows - processor_number * sub_rows
    both_halves = jnp.take(mixed, shard_of * (sub_rows // 2) + offsets // 2, axis=0)
    chosen = jnp.where(
        (offsets % 2 == 1)[:, :, None], both_halves[:, :, slab_width:], both_halves[:, :, :slab_width]
    )

    owner_list = owners[:, 0]
    preceding_rows = jnp.logical_and(
        owner_list[None, :] == owner_list[:, None], block_ids[None, :] < block_ids[:, None]
    )
    ranks = jnp.sum(preceding_rows.astype(jnp.int32), axis=1)
    slots = owner_list * CAPB + ranks
    placing = (jnp.arange(row_devices * CAPB, dtype=jnp.int32)[:, None] == slots[None, :]).astype(
        jnp.float32
    )
    bundled = jnp.einsum("kb,bps->kps", placing, chosen, precision=lax.Precision.HIGHEST)
    bundled = bundled.reshape(row_devices, CAPB, 2 * slab_width)
    arriving = lax.all_to_all(bundled, "rows", split_axis=0, concat_axis=0, tiled=True)
    received_rows = jnp.transpose(arriving, (1, 0, 2)).reshape(CAPB, row_devices * 2, slab_width)
    whole_rows = lax.all_gather(received_rows, "cols", axis=2, tiled=True)
    owned_total = jnp.sum((owner_list == processor_number).astype(jnp.int32))
    scalars = jnp.stack([lax.axis_index("cols").astype(jnp.int32), owned_total.astype(jnp.int32)])
    return cholesky_upper(scalars, whole_rows, slab_width)


def solution(mesh):
    in_specs = (P("cols", "rows"), P("rows"), P(), P())
    out_specs = P("rows", "cols", None)
    return jax.shard_map(
        per_device, mesh=mesh, in_specs=in_specs, out_specs=out_specs, check_vma=False
    )
```

```python
import math

import jax
import numpy as np
import jax.numpy as jnp
from jax import lax
from jax.experimental import pallas as pl
from jax.experimental.pallas import tpu as pltpu
from jax.sharding import PartitionSpec as P

HB = 128
SKETCH_ROW_COUNT = 256
CAPB = 4

PANEL = 32
STEP = 8


def cholesky_kernel(scalar_ref, rows_ref, out_ref, work_ref):
    blocks, samples, order = rows_ref.shape
    for b in range(blocks):
        gram = lax.dot_general(
            rows_ref[b], rows_ref[b], (((0,), (0,)), ((), ())),
            precision=lax.Precision.HIGHEST, preferred_element_type=jnp.float32,
        ) / samples
        diagonal = (
            lax.broadcasted_iota(jnp.int32, (order, order), 0)
            == lax.broadcasted_iota(jnp.int32, (order, order), 1)
        )
        identity = jnp.where(diagonal, 1.0, 0.0)
        work_ref[b] = jnp.where(b < scalar_ref[1], gram, identity)
    lane = lax.broadcasted_iota(jnp.int32, (blocks, 1, order), 2)
    sub_panel = lax.broadcasted_iota(jnp.int32, (blocks, PANEL, order), 1)
    for p in range(order // PANEL):
        base = p * PANEL
        panel = work_ref[:, base:base + PANEL, :]
        for first in range(0, PANEL, STEP):
            columns = [
                jnp.broadcast_to(panel[:, :, base + first + m:base + first + m + 1], panel.shape)
                for m in range(STEP)
            ]
            factor_rows, factor_columns = [], []
            for m in range(STEP):
                jj = first + m
                column = columns[m]
                row = panel[:, jj:jj + 1, :]
                for earlier in range(m):
                    coupling = factor_columns[earlier][:, jj:jj + 1, :]
                    column = column - factor_columns[earlier] * coupling
                    row = row - coupling * factor_rows[earlier]
                inverse_root = lax.rsqrt(column[:, jj:jj + 1, :])
                factor_rows.append(jnp.where(lane >= base + jj, row * inverse_root, 0.0))
                factor_columns.append(jnp.where(sub_panel > jj, column * inverse_root, 0.0))
            for m in range(STEP):
                panel = panel - factor_columns[m] * factor_rows[m]
            for m in range(STEP):
                panel = jnp.where(sub_panel == first + m, factor_rows[m], panel)
        if p + 1 < order // PANEL:
            for b in range(blocks):
                update = lax.dot_general(
                    panel[b], panel[b], (((0,), (0,)), ((), ())),
                    precision=lax.Precision.HIGHEST, preferred_element_type=jnp.float32,
                )
                work_ref[b, base + PANEL:, :] = work_ref[b, base + PANEL:, :] - update[base + PANEL:, :]
        work_ref[:, base:base + PANEL, :] = panel
    start = pl.multiple_of(scalar_ref[0] * out_ref.shape[1], out_ref.shape[1])
    for b in range(blocks):
        out_ref[b] = jnp.where(b < scalar_ref[1], work_ref[b, pl.ds(start, out_ref.shape[1]), :], 0.0)


def cholesky_upper(scalars, whole_rows, slab_width):
    blocks, samples, order = whole_rows.shape
    return pl.pallas_call(
        cholesky_kernel,
        out_shape=jax.ShapeDtypeStruct((blocks, slab_width, order), jnp.float32),
        grid_spec=pltpu.PrefetchScalarGridSpec(
            num_scalar_prefetch=1,
            grid=(1,),
            in_specs=[pl.BlockSpec(memory_space=pltpu.VMEM)],
            out_specs=pl.BlockSpec(memory_space=pltpu.VMEM),
            scratch_shapes=[pltpu.VMEM((blocks, order, order), jnp.float32)],
        ),
    )(scalars, whole_rows)


def local_mix_kernel(matrix_ref, signs_ref, table_ref, out_ref):
    slab_width = matrix_ref.shape[0]
    rows = out_ref.shape[1]
    groups = table_ref.shape[1] // rows

    def body(blk, carry):
        start = pl.multiple_of(blk * HB, HB)
        flips = (1 - 2 * signs_ref[:, pl.ds(start, HB)]).astype(jnp.float32)
        flipped = (matrix_ref[:, pl.ds(start, HB)].astype(jnp.float32) * flips).astype(jnp.bfloat16)
        for parity in range(2):
            mixed = lax.dot_general(
                table_ref[parity], flipped, (((1,), (1,)), ((), ())),
                preferred_element_type=jnp.float32,
            )
            for h in range(groups):
                out_ref[blk * groups + h, :, parity * slab_width:(parity + 1) * slab_width] = (
                    mixed[h * rows:(h + 1) * rows, :]
                )
        return carry

    lax.fori_loop(0, matrix_ref.shape[1] // HB, body, 0, unroll=True)


def local_mix(matrix, signs, table, row_devices):
    slab_width, shard_rows = matrix.shape
    sub_rows = shard_rows // row_devices
    return pl.pallas_call(
        local_mix_kernel,
        out_shape=jax.ShapeDtypeStruct((row_devices, sub_rows // 2, 2 * slab_width), jnp.float32),
        in_specs=[pl.BlockSpec(memory_space=pltpu.VMEM)] * 3,
        out_specs=pl.BlockSpec(memory_space=pltpu.VMEM),
    )(matrix, signs, table)


def walsh_sign_matrix(order):
    index_row = np.arange(order)
    parity = np.zeros((order, order), np.int64)
    for bit_place in range(order.bit_length() - 1):
        both = np.bitwise_and(index_row[:, None], index_row[None, :])
        parity = parity + np.bitwise_and(np.right_shift(both, bit_place), 1)
    return (1 - 2 * (parity % 2)).astype(np.float32)


def per_device(matrix, signs, samples, owners):
    slab_width = matrix.shape[0]
    shard_rows = matrix.shape[1]
    row_devices = lax.axis_size("rows")
    processor_number = lax.axis_index("rows")
    sub_rows = shard_rows // row_devices
    scale = 1.0 / math.sqrt(HB * row_devices)
    table = (walsh_sign_matrix(HB) * scale).reshape(HB // 2, 2, HB).transpose(1, 0, 2)
    outgoing = local_mix(matrix, signs.reshape(1, shard_rows), jnp.asarray(table, jnp.bfloat16), row_devices)
    received = lax.all_to_all(outgoing, "rows", split_axis=0, concat_axis=0, tiled=True)
    across = jnp.asarray(walsh_sign_matrix(row_devices))
    mixed = jnp.einsum(
        "st,tvl->vsl", across, received, precision=lax.Precision.HIGHEST
    ).reshape(row_devices * sub_rows // 2, 2 * slab_width)

    block_total = samples.shape[0]
    block_ids = jnp.arange(block_total, dtype=jnp.int32)
    first_q = jnp.mod(processor_number - block_ids, row_devices)
    picks = jnp.stack([first_q, first_q + row_devices], axis=1)
    sample_values = jnp.take_along_axis(samples, picks, axis=1)
    shard_of = picks // (samples.shape[1] // row_devices)
    offsets = sample_values - shard_of * shard_rows - processor_number * sub_rows
    both_halves = jnp.take(mixed, (offsets // 2) * row_devices + shard_of, axis=0)
    chosen = jnp.where(
        (offsets % 2 == 1)[:, :, None], both_halves[:, :, slab_width:], both_halves[:, :, :slab_width]
    )

    owner_list = owners[:, 0]
    preceding_rows = jnp.logical_and(
        owner_list[None, :] == owner_list[:, None], block_ids[None, :] < block_ids[:, None]
    )
    ranks = jnp.sum(preceding_rows.astype(jnp.int32), axis=1)
    slots = owner_list * CAPB + ranks
    placing = (jnp.arange(row_devices * CAPB, dtype=jnp.int32)[:, None] == slots[None, :]).astype(
        jnp.float32
    )
    bundled = jnp.einsum("kb,bps->kps", placing, chosen, precision=lax.Precision.HIGHEST)
    bundled = bundled.reshape(row_devices, CAPB, 2 * slab_width)
    arriving = lax.all_to_all(bundled, "rows", split_axis=0, concat_axis=0, tiled=True)
    received_rows = jnp.transpose(arriving, (1, 0, 2)).reshape(CAPB, row_devices * 2, slab_width)
    whole_rows = lax.all_gather(received_rows, "cols", axis=2, tiled=True)
    owned_total = jnp.sum((owner_list == processor_number).astype(jnp.int32))
    scalars = jnp.stack([lax.axis_index("cols").astype(jnp.int32), owned_total.astype(jnp.int32)])
    return cholesky_upper(scalars, whole_rows, slab_width)


def solution(mesh):
    in_specs = (P("cols", "rows"), P("rows"), P(), P())
    out_specs = P("rows", "cols", None)
    return jax.shard_map(
        per_device, mesh=mesh, in_specs=in_specs, out_specs=out_specs, check_vma=False
    )
```

```python
import math

import jax
import numpy as np
import jax.numpy as jnp
from jax import lax
from jax.experimental import pallas as pl
from jax.experimental.pallas import tpu as pltpu
from jax.sharding import PartitionSpec as P

HB = 128
SKETCH_ROW_COUNT = 256
CAPB = 4

PANEL = 32
STEP = 8


def cholesky_kernel(scalar_ref, rows_ref, out_ref, work_ref):
    cores, blocks, width, samples = rows_ref.shape
    order = cores * width
    for b in range(blocks):
        columns = jnp.concatenate([rows_ref[core, b] for core in range(cores)], axis=0)
        gram = lax.dot_general(
            columns, columns, (((1,), (1,)), ((), ())),
            precision=lax.Precision.HIGHEST, preferred_element_type=jnp.float32,
        ) / samples
        diagonal = (
            lax.broadcasted_iota(jnp.int32, (order, order), 0)
            == lax.broadcasted_iota(jnp.int32, (order, order), 1)
        )
        identity = jnp.where(diagonal, 1.0, 0.0)
        work_ref[b] = jnp.where(b < scalar_ref[1], gram, identity)
    lane = lax.broadcasted_iota(jnp.int32, (blocks, 1, order), 2)
    sub_panel = lax.broadcasted_iota(jnp.int32, (blocks, PANEL, order), 1)
    for p in range(order // PANEL):
        base = p * PANEL
        panel = work_ref[:, base:base + PANEL, :]
        for first in range(0, PANEL, STEP):
            columns = [
                jnp.broadcast_to(panel[:, :, base + first + m:base + first + m + 1], panel.shape)
                for m in range(STEP)
            ]
            factor_rows, factor_columns = [], []
            for m in range(STEP):
                jj = first + m
                column = columns[m]
                row = panel[:, jj:jj + 1, :]
                for earlier in range(m):
                    coupling = factor_columns[earlier][:, jj:jj + 1, :]
                    column = column - factor_columns[earlier] * coupling
                    row = row - coupling * factor_rows[earlier]
                inverse_root = lax.rsqrt(column[:, jj:jj + 1, :])
                factor_rows.append(jnp.where(lane >= base + jj, row * inverse_root, 0.0))
                factor_columns.append(jnp.where(sub_panel > jj, column * inverse_root, 0.0))
            for m in range(STEP):
                panel = panel - factor_columns[m] * factor_rows[m]
            for m in range(STEP):
                panel = jnp.where(sub_panel == first + m, factor_rows[m], panel)
        if p + 1 < order // PANEL:
            for b in range(blocks):
                update = lax.dot_general(
                    panel[b], panel[b], (((0,), (0,)), ((), ())),
                    precision=lax.Precision.HIGHEST, preferred_element_type=jnp.float32,
                )
                work_ref[b, base + PANEL:, :] = work_ref[b, base + PANEL:, :] - update[base + PANEL:, :]
        work_ref[:, base:base + PANEL, :] = panel
    start = pl.multiple_of(scalar_ref[0] * out_ref.shape[1], out_ref.shape[1])
    for b in range(blocks):
        out_ref[b] = jnp.where(b < scalar_ref[1], work_ref[b, pl.ds(start, out_ref.shape[1]), :], 0.0)


def cholesky_upper(scalars, whole_rows, slab_width):
    cores, blocks, width, samples = whole_rows.shape
    order = cores * width
    return pl.pallas_call(
        cholesky_kernel,
        out_shape=jax.ShapeDtypeStruct((blocks, slab_width, order), jnp.float32),
        grid_spec=pltpu.PrefetchScalarGridSpec(
            num_scalar_prefetch=1,
            grid=(1,),
            in_specs=[pl.BlockSpec(memory_space=pltpu.VMEM)],
            out_specs=pl.BlockSpec(memory_space=pltpu.VMEM),
            scratch_shapes=[pltpu.VMEM((blocks, order, order), jnp.float32)],
        ),
    )(scalars, whole_rows)


def local_mix_kernel(matrix_ref, signs_ref, table_ref, out_ref):
    slab_width = matrix_ref.shape[0]
    rows = out_ref.shape[1]
    groups = table_ref.shape[1] // rows

    def body(blk, carry):
        start = pl.multiple_of(blk * HB, HB)
        flips = (1 - 2 * signs_ref[:, pl.ds(start, HB)]).astype(jnp.float32)
        flipped = (matrix_ref[:, pl.ds(start, HB)].astype(jnp.float32) * flips).astype(jnp.bfloat16)
        for parity in range(2):
            mixed = lax.dot_general(
                table_ref[parity], flipped, (((1,), (1,)), ((), ())),
                preferred_element_type=jnp.float32,
            )
            for h in range(groups):
                out_ref[blk * groups + h, :, parity * slab_width:(parity + 1) * slab_width] = (
                    mixed[h * rows:(h + 1) * rows, :]
                )
        return carry

    lax.fori_loop(0, matrix_ref.shape[1] // HB, body, 0, unroll=True)


def local_mix(matrix, signs, table, row_devices):
    slab_width, shard_rows = matrix.shape
    sub_rows = shard_rows // row_devices
    return pl.pallas_call(
        local_mix_kernel,
        out_shape=jax.ShapeDtypeStruct((row_devices, sub_rows // 2, 2 * slab_width), jnp.float32),
        in_specs=[pl.BlockSpec(memory_space=pltpu.VMEM)] * 3,
        out_specs=pl.BlockSpec(memory_space=pltpu.VMEM),
    )(matrix, signs, table)


def walsh_sign_matrix(order):
    index_row = np.arange(order)
    parity = np.zeros((order, order), np.int64)
    for bit_place in range(order.bit_length() - 1):
        both = np.bitwise_and(index_row[:, None], index_row[None, :])
        parity = parity + np.bitwise_and(np.right_shift(both, bit_place), 1)
    return (1 - 2 * (parity % 2)).astype(np.float32)


def per_device(matrix, signs, samples, owners):
    slab_width = matrix.shape[0]
    shard_rows = matrix.shape[1]
    row_devices = lax.axis_size("rows")
    processor_number = lax.axis_index("rows")
    sub_rows = shard_rows // row_devices
    scale = 1.0 / math.sqrt(HB * row_devices)
    table = (walsh_sign_matrix(HB) * scale).reshape(HB // 2, 2, HB).transpose(1, 0, 2)
    outgoing = local_mix(matrix, signs.reshape(1, shard_rows), jnp.asarray(table, jnp.bfloat16), row_devices)
    received = lax.all_to_all(outgoing, "rows", split_axis=0, concat_axis=0, tiled=True)
    across = jnp.asarray(walsh_sign_matrix(row_devices))
    mixed = jnp.einsum(
        "st,tvl->vsl", across, received, precision=lax.Precision.HIGHEST
    ).reshape(row_devices * sub_rows // 2, 2 * slab_width)

    block_total = samples.shape[0]
    block_ids = jnp.arange(block_total, dtype=jnp.int32)
    first_q = jnp.mod(processor_number - block_ids, row_devices)
    picks = jnp.stack([first_q, first_q + row_devices], axis=1)
    sample_values = jnp.take_along_axis(samples, picks, axis=1)
    shard_of = picks // (samples.shape[1] // row_devices)
    offsets = sample_values - shard_of * shard_rows - processor_number * sub_rows
    both_halves = jnp.take(mixed, (offsets // 2) * row_devices + shard_of, axis=0)
    chosen = jnp.where(
        (offsets % 2 == 1)[:, :, None], both_halves[:, :, slab_width:], both_halves[:, :, :slab_width]
    )

    owner_list = owners[:, 0]
    preceding_rows = jnp.logical_and(
        owner_list[None, :] == owner_list[:, None], block_ids[None, :] < block_ids[:, None]
    )
    ranks = jnp.sum(preceding_rows.astype(jnp.int32), axis=1)
    slots = owner_list * CAPB + ranks
    placing = (jnp.arange(row_devices * CAPB, dtype=jnp.int32)[:, None] == slots[None, :]).astype(
        jnp.float32
    )
    bundled = jnp.einsum("kb,bps->kps", placing, chosen, precision=lax.Precision.HIGHEST)
    bundled = bundled.reshape(row_devices, CAPB, 2 * slab_width)
    arriving = lax.all_to_all(bundled, "rows", split_axis=0, concat_axis=0, tiled=True)
    received_rows = arriving.reshape(row_devices, CAPB, 2, slab_width).transpose(1, 3, 0, 2)
    received_rows = received_rows.reshape(CAPB, slab_width, row_devices * 2)
    whole_rows = lax.all_gather(received_rows, "cols", axis=0, tiled=False)
    owned_total = jnp.sum((owner_list == processor_number).astype(jnp.int32))
    scalars = jnp.stack([lax.axis_index("cols").astype(jnp.int32), owned_total.astype(jnp.int32)])
    return cholesky_upper(scalars, whole_rows, slab_width)


def solution(mesh):
    in_specs = (P("cols", "rows"), P("rows"), P(), P())
    out_specs = P("rows", "cols", None)
    return jax.shard_map(
        per_device, mesh=mesh, in_specs=in_specs, out_specs=out_specs, check_vma=False
    )
```

```python
import math

import jax
import numpy as np
import jax.numpy as jnp
from jax import lax
from jax.experimental import pallas as pl
from jax.experimental.pallas import tpu as pltpu
from jax.sharding import PartitionSpec as P

HB = 128
SKETCH_ROW_COUNT = 256
CAPB = 4

PANEL = 32
STEP = 8


def cholesky_kernel(scalar_ref, rows_ref, out_ref, work_ref):
    cores, blocks, width, samples = rows_ref.shape
    order = cores * width
    for b in range(blocks):
        columns = jnp.concatenate([rows_ref[core, b] for core in range(cores)], axis=0)
        gram = lax.dot_general(
            columns, columns, (((1,), (1,)), ((), ())),
            precision=lax.Precision.HIGHEST, preferred_element_type=jnp.float32,
        ) / samples
        diagonal = (
            lax.broadcasted_iota(jnp.int32, (order, order), 0)
            == lax.broadcasted_iota(jnp.int32, (order, order), 1)
        )
        identity = jnp.where(diagonal, 1.0, 0.0)
        work_ref[b] = jnp.where(b < scalar_ref[1], gram, identity)
    lane = lax.broadcasted_iota(jnp.int32, (blocks, 1, order), 2)
    sub_panel = lax.broadcasted_iota(jnp.int32, (blocks, PANEL, order), 1)
    for p in range(order // PANEL):
        base = p * PANEL
        panel = work_ref[:, base:base + PANEL, :]
        for first in range(0, PANEL, STEP):
            columns = [
                jnp.broadcast_to(panel[:, :, base + first + m:base + first + m + 1], panel.shape)
                for m in range(STEP)
            ]
            factor_rows, factor_columns = [], []
            for m in range(STEP):
                jj = first + m
                column = columns[m]
                row = panel[:, jj:jj + 1, :]
                for earlier in range(m):
                    coupling = factor_columns[earlier][:, jj:jj + 1, :]
                    column = column - factor_columns[earlier] * coupling
                    row = row - coupling * factor_rows[earlier]
                inverse_root = lax.rsqrt(column[:, jj:jj + 1, :])
                factor_rows.append(jnp.where(lane >= base + jj, row * inverse_root, 0.0))
                factor_columns.append(jnp.where(sub_panel > jj, column * inverse_root, 0.0))
            for m in range(STEP):
                panel = panel - factor_columns[m] * factor_rows[m]
            for m in range(STEP):
                panel = jnp.where(sub_panel == first + m, factor_rows[m], panel)
        if p + 1 < order // PANEL:
            for b in range(blocks):
                update = lax.dot_general(
                    panel[b], panel[b], (((0,), (0,)), ((), ())),
                    precision=lax.Precision.HIGHEST, preferred_element_type=jnp.float32,
                )
                work_ref[b, base + PANEL:, :] = work_ref[b, base + PANEL:, :] - update[base + PANEL:, :]
        work_ref[:, base:base + PANEL, :] = panel
    start = pl.multiple_of(scalar_ref[0] * out_ref.shape[1], out_ref.shape[1])
    for b in range(blocks):
        out_ref[b] = jnp.where(b < scalar_ref[1], work_ref[b, pl.ds(start, out_ref.shape[1]), :], 0.0)


def cholesky_upper(scalars, whole_rows, slab_width):
    cores, blocks, width, samples = whole_rows.shape
    order = cores * width
    return pl.pallas_call(
        cholesky_kernel,
        out_shape=jax.ShapeDtypeStruct((blocks, slab_width, order), jnp.float32),
        grid_spec=pltpu.PrefetchScalarGridSpec(
            num_scalar_prefetch=1,
            grid=(1,),
            in_specs=[pl.BlockSpec(memory_space=pltpu.VMEM)],
            out_specs=pl.BlockSpec(memory_space=pltpu.VMEM),
            scratch_shapes=[pltpu.VMEM((blocks, order, order), jnp.float32)],
        ),
    )(scalars, whole_rows)


def local_mix_kernel(matrix_ref, signs_ref, table_ref, out_ref):
    slab_width = matrix_ref.shape[0]
    rows = out_ref.shape[1]
    groups = table_ref.shape[0] // (2 * rows)

    def body(blk, carry):
        start = pl.multiple_of(blk * HB, HB)
        flips = (1 - 2 * signs_ref[:, pl.ds(start, HB)]).astype(jnp.float32)
        flipped = (matrix_ref[:, pl.ds(start, HB)].astype(jnp.float32) * flips).astype(jnp.bfloat16)
        mixed = lax.dot_general(
            table_ref[...], flipped, (((1,), (1,)), ((), ())),
            preferred_element_type=jnp.float32,
        )
        for parity in range(2):
            for h in range(groups):
                first = parity * groups * rows + h * rows
                out_ref[blk * groups + h, :, parity * slab_width:(parity + 1) * slab_width] = (
                    mixed[first:first + rows, :]
                )
        return carry

    lax.fori_loop(0, matrix_ref.shape[1] // HB, body, 0, unroll=True)


def local_mix(matrix, signs, table, row_devices):
    slab_width, shard_rows = matrix.shape
    sub_rows = shard_rows // row_devices
    return pl.pallas_call(
        local_mix_kernel,
        out_shape=jax.ShapeDtypeStruct((row_devices, sub_rows // 2, 2 * slab_width), jnp.float32),
        in_specs=[pl.BlockSpec(memory_space=pltpu.VMEM)] * 3,
        out_specs=pl.BlockSpec(memory_space=pltpu.VMEM),
    )(matrix, signs, table)


def walsh_sign_matrix(order):
    index_row = np.arange(order)
    parity = np.zeros((order, order), np.int64)
    for bit_place in range(order.bit_length() - 1):
        both = np.bitwise_and(index_row[:, None], index_row[None, :])
        parity = parity + np.bitwise_and(np.right_shift(both, bit_place), 1)
    return (1 - 2 * (parity % 2)).astype(np.float32)


def per_device(matrix, signs, samples, owners):
    slab_width = matrix.shape[0]
    shard_rows = matrix.shape[1]
    row_devices = lax.axis_size("rows")
    processor_number = lax.axis_index("rows")
    sub_rows = shard_rows // row_devices
    scale = 1.0 / math.sqrt(HB * row_devices)
    table = (walsh_sign_matrix(HB) * scale).reshape(HB // 2, 2, HB).transpose(1, 0, 2).reshape(HB, HB)
    outgoing = local_mix(matrix, signs.reshape(1, shard_rows), jnp.asarray(table, jnp.bfloat16), row_devices)
    received = lax.all_to_all(outgoing, "rows", split_axis=0, concat_axis=0, tiled=True)
    across = jnp.asarray(walsh_sign_matrix(row_devices))
    mixed = jnp.einsum(
        "st,tvl->vsl", across, received, precision=lax.Precision.HIGHEST
    ).reshape(row_devices * sub_rows // 2, 2 * slab_width)

    block_total = samples.shape[0]
    block_ids = jnp.arange(block_total, dtype=jnp.int32)
    first_q = jnp.mod(processor_number - block_ids, row_devices)
    picks = jnp.stack([first_q, first_q + row_devices], axis=1)
    sample_values = jnp.take_along_axis(samples, picks, axis=1)
    shard_of = picks // (samples.shape[1] // row_devices)
    offsets = sample_values - shard_of * shard_rows - processor_number * sub_rows
    both_halves = jnp.take(mixed, (offsets // 2) * row_devices + shard_of, axis=0)
    chosen = jnp.where(
        (offsets % 2 == 1)[:, :, None], both_halves[:, :, slab_width:], both_halves[:, :, :slab_width]
    )

    owner_list = owners[:, 0]
    preceding_rows = jnp.logical_and(
        owner_list[None, :] == owner_list[:, None], block_ids[None, :] < block_ids[:, None]
    )
    ranks = jnp.sum(preceding_rows.astype(jnp.int32), axis=1)
    slots = owner_list * CAPB + ranks
    placing = (jnp.arange(row_devices * CAPB, dtype=jnp.int32)[:, None] == slots[None, :]).astype(
        jnp.float32
    )
    bundled = jnp.einsum("kb,bps->kps", placing, chosen, precision=lax.Precision.HIGHEST)
    bundled = bundled.reshape(row_devices, CAPB, 2 * slab_width)
    arriving = lax.all_to_all(bundled, "rows", split_axis=0, concat_axis=0, tiled=True)
    received_rows = arriving.reshape(row_devices, CAPB, 2, slab_width).transpose(1, 3, 0, 2)
    received_rows = received_rows.reshape(CAPB, slab_width, row_devices * 2)
    whole_rows = lax.all_gather(received_rows, "cols", axis=0, tiled=False)
    owned_total = jnp.sum((owner_list == processor_number).astype(jnp.int32))
    scalars = jnp.stack([lax.axis_index("cols").astype(jnp.int32), owned_total.astype(jnp.int32)])
    return cholesky_upper(scalars, whole_rows, slab_width)


def solution(mesh):
    in_specs = (P("cols", "rows"), P("rows"), P(), P())
    out_specs = P("rows", "cols", None)
    return jax.shard_map(
        per_device, mesh=mesh, in_specs=in_specs, out_specs=out_specs, check_vma=False
    )
```

```python
import math

import jax
import numpy as np
import jax.numpy as jnp
from jax import lax
from jax.experimental import pallas as pl
from jax.experimental.pallas import tpu as pltpu
from jax.sharding import PartitionSpec as P

HB = 128
SKETCH_ROW_COUNT = 256
CAPB = 4

PANEL = 32
STEP = 8


def cholesky_kernel(scalar_ref, own_ref, other_ref, out_ref, work_ref):
    blocks, width, samples = own_ref.shape
    order = 2 * width
    for b in range(blocks):
        first = jnp.where(scalar_ref[0] == 0, own_ref[b], other_ref[b])
        second = jnp.where(scalar_ref[0] == 0, other_ref[b], own_ref[b])
        columns = jnp.concatenate([first, second], axis=0)
        gram = lax.dot_general(
            columns, columns, (((1,), (1,)), ((), ())),
            precision=lax.Precision.HIGHEST, preferred_element_type=jnp.float32,
        ) / samples
        diagonal = (
            lax.broadcasted_iota(jnp.int32, (order, order), 0)
            == lax.broadcasted_iota(jnp.int32, (order, order), 1)
        )
        identity = jnp.where(diagonal, 1.0, 0.0)
        work_ref[b] = jnp.where(b < scalar_ref[1], gram, identity)
    lane = lax.broadcasted_iota(jnp.int32, (blocks, 1, order), 2)
    sub_panel = lax.broadcasted_iota(jnp.int32, (blocks, PANEL, order), 1)
    for p in range(order // PANEL):
        base = p * PANEL
        panel = work_ref[:, base:base + PANEL, :]
        for first in range(0, PANEL, STEP):
            columns = [
                jnp.broadcast_to(panel[:, :, base + first + m:base + first + m + 1], panel.shape)
                for m in range(STEP)
            ]
            factor_rows, factor_columns = [], []
            for m in range(STEP):
                jj = first + m
                column = columns[m]
                row = panel[:, jj:jj + 1, :]
                for earlier in range(m):
                    coupling = factor_columns[earlier][:, jj:jj + 1, :]
                    column = column - factor_columns[earlier] * coupling
                    row = row - coupling * factor_rows[earlier]
                inverse_root = lax.rsqrt(column[:, jj:jj + 1, :])
                factor_rows.append(jnp.where(lane >= base + jj, row * inverse_root, 0.0))
                factor_columns.append(jnp.where(sub_panel > jj, column * inverse_root, 0.0))
            for m in range(STEP):
                panel = panel - factor_columns[m] * factor_rows[m]
            for m in range(STEP):
                panel = jnp.where(sub_panel == first + m, factor_rows[m], panel)
        if p + 1 < order // PANEL:
            for b in range(blocks):
                update = lax.dot_general(
                    panel[b], panel[b], (((0,), (0,)), ((), ())),
                    precision=lax.Precision.HIGHEST, preferred_element_type=jnp.float32,
                )
                work_ref[b, base + PANEL:, :] = work_ref[b, base + PANEL:, :] - update[base + PANEL:, :]
        work_ref[:, base:base + PANEL, :] = panel
    start = pl.multiple_of(scalar_ref[0] * out_ref.shape[1], out_ref.shape[1])
    for b in range(blocks):
        out_ref[b] = jnp.where(b < scalar_ref[1], work_ref[b, pl.ds(start, out_ref.shape[1]), :], 0.0)


def cholesky_upper(scalars, own_rows, other_rows, slab_width):
    blocks, width, samples = own_rows.shape
    order = 2 * width
    return pl.pallas_call(
        cholesky_kernel,
        out_shape=jax.ShapeDtypeStruct((blocks, slab_width, order), jnp.float32),
        grid_spec=pltpu.PrefetchScalarGridSpec(
            num_scalar_prefetch=1,
            grid=(1,),
            in_specs=[pl.BlockSpec(memory_space=pltpu.VMEM)] * 2,
            out_specs=pl.BlockSpec(memory_space=pltpu.VMEM),
            scratch_shapes=[pltpu.VMEM((blocks, order, order), jnp.float32)],
        ),
    )(scalars, own_rows, other_rows)


def local_mix_kernel(matrix_ref, signs_ref, table_ref, out_ref):
    slab_width = matrix_ref.shape[0]
    rows = out_ref.shape[1]
    groups = table_ref.shape[0] // (2 * rows)

    def body(blk, carry):
        start = pl.multiple_of(blk * HB, HB)
        flips = (1 - 2 * signs_ref[:, pl.ds(start, HB)]).astype(jnp.float32)
        flipped = (matrix_ref[:, pl.ds(start, HB)].astype(jnp.float32) * flips).astype(jnp.bfloat16)
        mixed = lax.dot_general(
            table_ref[...], flipped, (((1,), (1,)), ((), ())),
            preferred_element_type=jnp.float32,
        )
        for parity in range(2):
            for h in range(groups):
                first = parity * groups * rows + h * rows
                out_ref[blk * groups + h, :, parity * slab_width:(parity + 1) * slab_width] = (
                    mixed[first:first + rows, :]
                )
        return carry

    lax.fori_loop(0, matrix_ref.shape[1] // HB, body, 0, unroll=True)


def local_mix(matrix, signs, table, row_devices):
    slab_width, shard_rows = matrix.shape
    sub_rows = shard_rows // row_devices
    return pl.pallas_call(
        local_mix_kernel,
        out_shape=jax.ShapeDtypeStruct((row_devices, sub_rows // 2, 2 * slab_width), jnp.float32),
        in_specs=[pl.BlockSpec(memory_space=pltpu.VMEM)] * 3,
        out_specs=pl.BlockSpec(memory_space=pltpu.VMEM),
    )(matrix, signs, table)


def walsh_sign_matrix(order):
    index_row = np.arange(order)
    parity = np.zeros((order, order), np.int64)
    for bit_place in range(order.bit_length() - 1):
        both = np.bitwise_and(index_row[:, None], index_row[None, :])
        parity = parity + np.bitwise_and(np.right_shift(both, bit_place), 1)
    return (1 - 2 * (parity % 2)).astype(np.float32)


def per_device(matrix, signs, samples, owners):
    slab_width = matrix.shape[0]
    shard_rows = matrix.shape[1]
    row_devices = lax.axis_size("rows")
    processor_number = lax.axis_index("rows")
    sub_rows = shard_rows // row_devices
    scale = 1.0 / math.sqrt(HB * row_devices)
    table = (walsh_sign_matrix(HB) * scale).reshape(HB // 2, 2, HB).transpose(1, 0, 2).reshape(HB, HB)
    outgoing = local_mix(matrix, signs.reshape(1, shard_rows), jnp.asarray(table, jnp.bfloat16), row_devices)
    received = lax.all_to_all(outgoing, "rows", split_axis=0, concat_axis=0, tiled=True)
    across = jnp.asarray(walsh_sign_matrix(row_devices))
    mixed = jnp.einsum(
        "st,tvl->vsl", across, received, precision=lax.Precision.HIGHEST
    ).reshape(row_devices * sub_rows // 2, 2 * slab_width)

    block_total = samples.shape[0]
    block_ids = jnp.arange(block_total, dtype=jnp.int32)
    first_q = jnp.mod(processor_number - block_ids, row_devices)
    picks = jnp.stack([first_q, first_q + row_devices], axis=1)
    sample_values = jnp.take_along_axis(samples, picks, axis=1)
    shard_of = picks // (samples.shape[1] // row_devices)
    offsets = sample_values - shard_of * shard_rows - processor_number * sub_rows
    both_halves = jnp.take(mixed, (offsets // 2) * row_devices + shard_of, axis=0)
    chosen = jnp.where(
        (offsets % 2 == 1)[:, :, None], both_halves[:, :, slab_width:], both_halves[:, :, :slab_width]
    )

    owner_list = owners[:, 0]
    preceding_rows = jnp.logical_and(
        owner_list[None, :] == owner_list[:, None], block_ids[None, :] < block_ids[:, None]
    )
    ranks = jnp.sum(preceding_rows.astype(jnp.int32), axis=1)
    slots = owner_list * CAPB + ranks
    placing = (jnp.arange(row_devices * CAPB, dtype=jnp.int32)[:, None] == slots[None, :]).astype(
        jnp.float32
    )
    bundled = jnp.einsum("kb,bps->kps", placing, chosen, precision=lax.Precision.HIGHEST)
    bundled = bundled.reshape(row_devices, CAPB, 2 * slab_width)
    arriving = lax.all_to_all(bundled, "rows", split_axis=0, concat_axis=0, tiled=True)
    received_rows = arriving.reshape(row_devices, CAPB, 2, slab_width).transpose(1, 3, 0, 2)
    received_rows = received_rows.reshape(CAPB, slab_width, row_devices * 2)
    other_rows = lax.ppermute(received_rows, "cols", [(0, 1), (1, 0)])
    owned_total = jnp.sum((owner_list == processor_number).astype(jnp.int32))
    scalars = jnp.stack([lax.axis_index("cols").astype(jnp.int32), owned_total.astype(jnp.int32)])
    return cholesky_upper(scalars, received_rows, other_rows, slab_width)


def solution(mesh):
    in_specs = (P("cols", "rows"), P("rows"), P(), P())
    out_specs = P("rows", "cols", None)
    return jax.shard_map(
        per_device, mesh=mesh, in_specs=in_specs, out_specs=out_specs, check_vma=False
    )
```

```python
import math

import jax
import numpy as np
import jax.numpy as jnp
from jax import lax
from jax.experimental import pallas as pl
from jax.experimental.pallas import tpu as pltpu
from jax.sharding import PartitionSpec as P

HB = 128
SKETCH_ROW_COUNT = 256
CAPB = 4

PANEL = 32
STEP = 8


def cholesky_kernel(scalar_ref, owners_ref, own_ref, other_ref, out_ref, work_ref):
    blocks, width, samples = own_ref.shape
    order = 2 * width
    owned = jnp.sum(jnp.where(owners_ref[...] == scalar_ref[1], 1, 0))
    for b in range(blocks):
        first = jnp.where(scalar_ref[0] == 0, own_ref[b], other_ref[b])
        second = jnp.where(scalar_ref[0] == 0, other_ref[b], own_ref[b])
        columns = jnp.concatenate([first, second], axis=0)
        gram = lax.dot_general(
            columns, columns, (((1,), (1,)), ((), ())),
            precision=lax.Precision.HIGHEST, preferred_element_type=jnp.float32,
        ) / samples
        diagonal = (
            lax.broadcasted_iota(jnp.int32, (order, order), 0)
            == lax.broadcasted_iota(jnp.int32, (order, order), 1)
        )
        identity = jnp.where(diagonal, 1.0, 0.0)
        work_ref[b] = jnp.where(b < owned, gram, identity)
    lane = lax.broadcasted_iota(jnp.int32, (blocks, 1, order), 2)
    sub_panel = lax.broadcasted_iota(jnp.int32, (blocks, PANEL, order), 1)
    for p in range(order // PANEL):
        base = p * PANEL
        panel = work_ref[:, base:base + PANEL, :]
        for first in range(0, PANEL, STEP):
            columns = [
                jnp.broadcast_to(panel[:, :, base + first + m:base + first + m + 1], panel.shape)
                for m in range(STEP)
            ]
            factor_rows, factor_columns = [], []
            for m in range(STEP):
                jj = first + m
                column = columns[m]
                row = panel[:, jj:jj + 1, :]
                for earlier in range(m):
                    coupling = factor_columns[earlier][:, jj:jj + 1, :]
                    column = column - factor_columns[earlier] * coupling
                    row = row - coupling * factor_rows[earlier]
                inverse_root = lax.rsqrt(column[:, jj:jj + 1, :])
                factor_rows.append(jnp.where(lane >= base + jj, row * inverse_root, 0.0))
                factor_columns.append(jnp.where(sub_panel > jj, column * inverse_root, 0.0))
            for m in range(STEP):
                panel = panel - factor_columns[m] * factor_rows[m]
            for m in range(STEP):
                panel = jnp.where(sub_panel == first + m, factor_rows[m], panel)
        if p + 1 < order // PANEL:
            for b in range(blocks):
                update = lax.dot_general(
                    panel[b], panel[b], (((0,), (0,)), ((), ())),
                    precision=lax.Precision.HIGHEST, preferred_element_type=jnp.float32,
                )
                work_ref[b, base + PANEL:, :] = work_ref[b, base + PANEL:, :] - update[base + PANEL:, :]
        work_ref[:, base:base + PANEL, :] = panel
    start = pl.multiple_of(scalar_ref[0] * out_ref.shape[1], out_ref.shape[1])
    for b in range(blocks):
        out_ref[b] = jnp.where(b < owned, work_ref[b, pl.ds(start, out_ref.shape[1]), :], 0.0)


def cholesky_upper(scalars, owners, own_rows, other_rows, slab_width):
    blocks, width, samples = own_rows.shape
    order = 2 * width
    return pl.pallas_call(
        cholesky_kernel,
        out_shape=jax.ShapeDtypeStruct((blocks, slab_width, order), jnp.float32),
        grid_spec=pltpu.PrefetchScalarGridSpec(
            num_scalar_prefetch=1,
            grid=(1,),
            in_specs=[pl.BlockSpec(memory_space=pltpu.VMEM)] * 3,
            out_specs=pl.BlockSpec(memory_space=pltpu.VMEM),
            scratch_shapes=[pltpu.VMEM((blocks, order, order), jnp.float32)],
        ),
    )(scalars, owners, own_rows, other_rows)


def local_mix_kernel(matrix_ref, signs_ref, table_ref, out_ref):
    slab_width = matrix_ref.shape[0]
    rows = out_ref.shape[1]
    groups = table_ref.shape[0] // (2 * rows)

    def body(blk, carry):
        start = pl.multiple_of(blk * HB, HB)
        flips = (1 - 2 * signs_ref[:, pl.ds(start, HB)]).astype(jnp.float32)
        flipped = (matrix_ref[:, pl.ds(start, HB)].astype(jnp.float32) * flips).astype(jnp.bfloat16)
        mixed = lax.dot_general(
            table_ref[...], flipped, (((1,), (1,)), ((), ())),
            preferred_element_type=jnp.float32,
        )
        for parity in range(2):
            for h in range(groups):
                first = parity * groups * rows + h * rows
                out_ref[blk * groups + h, :, parity * slab_width:(parity + 1) * slab_width] = (
                    mixed[first:first + rows, :]
                )
        return carry

    lax.fori_loop(0, matrix_ref.shape[1] // HB, body, 0, unroll=True)


def local_mix(matrix, signs, table, row_devices):
    slab_width, shard_rows = matrix.shape
    sub_rows = shard_rows // row_devices
    return pl.pallas_call(
        local_mix_kernel,
        out_shape=jax.ShapeDtypeStruct((row_devices, sub_rows // 2, 2 * slab_width), jnp.float32),
        in_specs=[pl.BlockSpec(memory_space=pltpu.VMEM)] * 3,
        out_specs=pl.BlockSpec(memory_space=pltpu.VMEM),
    )(matrix, signs, table)


def walsh_sign_matrix(order):
    index_row = np.arange(order)
    parity = np.zeros((order, order), np.int64)
    for bit_place in range(order.bit_length() - 1):
        both = np.bitwise_and(index_row[:, None], index_row[None, :])
        parity = parity + np.bitwise_and(np.right_shift(both, bit_place), 1)
    return (1 - 2 * (parity % 2)).astype(np.float32)


def per_device(matrix, signs, samples, owners):
    slab_width = matrix.shape[0]
    shard_rows = matrix.shape[1]
    row_devices = lax.axis_size("rows")
    processor_number = lax.axis_index("rows")
    sub_rows = shard_rows // row_devices
    scale = 1.0 / math.sqrt(HB * row_devices)
    table = (walsh_sign_matrix(HB) * scale).reshape(HB // 2, 2, HB).transpose(1, 0, 2).reshape(HB, HB)
    outgoing = local_mix(matrix, signs.reshape(1, shard_rows), jnp.asarray(table, jnp.bfloat16), row_devices)
    received = lax.all_to_all(outgoing, "rows", split_axis=0, concat_axis=0, tiled=True)
    across = jnp.asarray(walsh_sign_matrix(row_devices))
    mixed = jnp.einsum(
        "st,tvl->vsl", across, received, precision=lax.Precision.HIGHEST
    ).reshape(row_devices * sub_rows // 2, 2 * slab_width)

    block_total = samples.shape[0]
    block_ids = jnp.arange(block_total, dtype=jnp.int32)
    first_q = jnp.mod(processor_number - block_ids, row_devices)
    picks = jnp.stack([first_q, first_q + row_devices], axis=1)
    sample_values = jnp.take_along_axis(samples, picks, axis=1)
    shard_of = picks // (samples.shape[1] // row_devices)
    offsets = sample_values - shard_of * shard_rows - processor_number * sub_rows
    both_halves = jnp.take(mixed, (offsets // 2) * row_devices + shard_of, axis=0)
    chosen = jnp.where(
        (offsets % 2 == 1)[:, :, None], both_halves[:, :, slab_width:], both_halves[:, :, :slab_width]
    )

    owner_list = owners[:, 0]
    preceding_rows = jnp.logical_and(
        owner_list[None, :] == owner_list[:, None], block_ids[None, :] < block_ids[:, None]
    )
    ranks = jnp.sum(preceding_rows.astype(jnp.int32), axis=1)
    slots = owner_list * CAPB + ranks
    placing = (jnp.arange(row_devices * CAPB, dtype=jnp.int32)[:, None] == slots[None, :]).astype(
        jnp.float32
    )
    bundled = jnp.einsum("kb,bps->kps", placing, chosen, precision=lax.Precision.HIGHEST)
    bundled = bundled.reshape(row_devices, CAPB, 2 * slab_width)
    arriving = lax.all_to_all(bundled, "rows", split_axis=0, concat_axis=0, tiled=True)
    received_rows = arriving.reshape(row_devices, CAPB, 2, slab_width).transpose(1, 3, 0, 2)
    received_rows = received_rows.reshape(CAPB, slab_width, row_devices * 2)
    other_rows = lax.ppermute(received_rows, "cols", [(0, 1), (1, 0)])
    scalars = jnp.stack([lax.axis_index("cols").astype(jnp.int32), processor_number.astype(jnp.int32)])
    owner_rows = owner_list.reshape(block_total // HB, HB)
    return cholesky_upper(scalars, owner_rows, received_rows, other_rows, slab_width)


def solution(mesh):
    in_specs = (P("cols", "rows"), P("rows"), P(), P())
    out_specs = P("rows", "cols", None)
    return jax.shard_map(
        per_device, mesh=mesh, in_specs=in_specs, out_specs=out_specs, check_vma=False
    )
```

```python
import math

import jax
import numpy as np
import jax.numpy as jnp
from jax import lax
from jax.experimental import pallas as pl
from jax.experimental.pallas import tpu as pltpu
from jax.sharding import PartitionSpec as P

HB = 128
SKETCH_ROW_COUNT = 256
CAPB = 4

PANEL = 32
STEP = 8


def cholesky_kernel(scalar_ref, own_ref, other_ref, out_ref, work_ref):
    blocks, width, samples = own_ref.shape
    order = 2 * width
    for b in range(blocks):
        first = jnp.where(scalar_ref[0] == 0, own_ref[b], other_ref[b])
        second = jnp.where(scalar_ref[0] == 0, other_ref[b], own_ref[b])
        columns = jnp.concatenate([first, second], axis=0)
        gram = lax.dot_general(
            columns, columns, (((1,), (1,)), ((), ())),
            precision=lax.Precision.HIGHEST, preferred_element_type=jnp.float32,
        ) / samples
        diagonal = (
            lax.broadcasted_iota(jnp.int32, (order, order), 0)
            == lax.broadcasted_iota(jnp.int32, (order, order), 1)
        )
        identity = jnp.where(diagonal, 1.0, 0.0)
        work_ref[b] = jnp.where(b < scalar_ref[1], gram, identity)
    lane = lax.broadcasted_iota(jnp.int32, (blocks, 1, order), 2)
    sub_panel = lax.broadcasted_iota(jnp.int32, (blocks, PANEL, order), 1)
    for p in range(order // PANEL):
        base = p * PANEL
        panel = work_ref[:, base:base + PANEL, :]
        for first in range(0, PANEL, STEP):
            columns = [
                jnp.broadcast_to(panel[:, :, base + first + m:base + first + m + 1], panel.shape)
                for m in range(STEP)
            ]
            factor_rows, factor_columns = [], []
            for m in range(STEP):
                jj = first + m
                column = columns[m]
                row = panel[:, jj:jj + 1, :]
                for earlier in range(m):
                    coupling = factor_columns[earlier][:, jj:jj + 1, :]
                    column = column - factor_columns[earlier] * coupling
                    row = row - coupling * factor_rows[earlier]
                inverse_root = lax.rsqrt(column[:, jj:jj + 1, :])
                factor_rows.append(jnp.where(lane >= base + jj, row * inverse_root, 0.0))
                factor_columns.append(jnp.where(sub_panel > jj, column * inverse_root, 0.0))
            for m in range(STEP):
                panel = panel - factor_columns[m] * factor_rows[m]
            for m in range(STEP):
                panel = jnp.where(sub_panel == first + m, factor_rows[m], panel)
        if p + 1 < order // PANEL:
            for b in range(blocks):
                update = lax.dot_general(
                    panel[b], panel[b], (((0,), (0,)), ((), ())),
                    precision=lax.Precision.HIGHEST, preferred_element_type=jnp.float32,
                )
                work_ref[b, base + PANEL:, :] = work_ref[b, base + PANEL:, :] - update[base + PANEL:, :]
        work_ref[:, base:base + PANEL, :] = panel
    start = pl.multiple_of(scalar_ref[0] * out_ref.shape[1], out_ref.shape[1])
    for b in range(blocks):
        out_ref[b] = jnp.where(b < scalar_ref[1], work_ref[b, pl.ds(start, out_ref.shape[1]), :], 0.0)


def cholesky_upper(scalars, own_rows, other_rows, slab_width):
    blocks, width, samples = own_rows.shape
    order = 2 * width
    return pl.pallas_call(
        cholesky_kernel,
        out_shape=jax.ShapeDtypeStruct((blocks, slab_width, order), jnp.float32),
        grid_spec=pltpu.PrefetchScalarGridSpec(
            num_scalar_prefetch=1,
            grid=(1,),
            in_specs=[pl.BlockSpec(memory_space=pltpu.VMEM)] * 2,
            out_specs=pl.BlockSpec(memory_space=pltpu.VMEM),
            scratch_shapes=[pltpu.VMEM((blocks, order, order), jnp.float32)],
        ),
    )(scalars, own_rows, other_rows)


def local_mix_kernel(matrix_ref, signs_ref, table_ref, out_ref):
    slab_width = matrix_ref.shape[0]
    rows = out_ref.shape[1]
    groups = table_ref.shape[0] // (2 * rows)

    def body(blk, carry):
        start = pl.multiple_of(blk * HB, HB)
        flips = (1 - 2 * signs_ref[:, pl.ds(start, HB)]).astype(jnp.float32)
        flipped = (matrix_ref[:, pl.ds(start, HB)].astype(jnp.float32) * flips).astype(jnp.bfloat16)
        mixed = lax.dot_general(
            table_ref[...], flipped, (((1,), (1,)), ((), ())),
            preferred_element_type=jnp.float32,
        )
        for parity in range(2):
            for h in range(groups):
                first = parity * groups * rows + h * rows
                out_ref[blk * groups + h, :, parity * slab_width:(parity + 1) * slab_width] = (
                    mixed[first:first + rows, :]
                )
        return carry

    lax.fori_loop(0, matrix_ref.shape[1] // HB, body, 0, unroll=True)


def local_mix(matrix, signs, table, row_devices):
    slab_width, shard_rows = matrix.shape
    sub_rows = shard_rows // row_devices
    return pl.pallas_call(
        local_mix_kernel,
        out_shape=jax.ShapeDtypeStruct((row_devices, sub_rows // 2, 2 * slab_width), jnp.float32),
        in_specs=[pl.BlockSpec(memory_space=pltpu.VMEM)] * 3,
        out_specs=pl.BlockSpec(memory_space=pltpu.VMEM),
    )(matrix, signs, table)


def walsh_sign_matrix(order):
    index_row = np.arange(order)
    parity = np.zeros((order, order), np.int64)
    for bit_place in range(order.bit_length() - 1):
        both = np.bitwise_and(index_row[:, None], index_row[None, :])
        parity = parity + np.bitwise_and(np.right_shift(both, bit_place), 1)
    return (1 - 2 * (parity % 2)).astype(np.float32)


def per_device(matrix, signs, samples, owners):
    slab_width = matrix.shape[0]
    shard_rows = matrix.shape[1]
    row_devices = lax.axis_size("rows")
    processor_number = lax.axis_index("rows")
    sub_rows = shard_rows // row_devices
    scale = 1.0 / math.sqrt(HB * row_devices)
    table = (walsh_sign_matrix(HB) * scale).reshape(HB // 2, 2, HB).transpose(1, 0, 2).reshape(HB, HB)
    outgoing = local_mix(matrix, signs.reshape(1, shard_rows), jnp.asarray(table, jnp.bfloat16), row_devices)
    received = lax.all_to_all(outgoing, "rows", split_axis=0, concat_axis=0, tiled=True)
    across = jnp.asarray(walsh_sign_matrix(row_devices))
    mixed = jnp.einsum(
        "st,tvl->vsl", across, received, precision=lax.Precision.HIGHEST
    ).reshape(row_devices * sub_rows // 2, 2 * slab_width)

    block_total = samples.shape[0]
    block_ids = jnp.arange(block_total, dtype=jnp.int32)
    first_q = jnp.mod(processor_number - block_ids, row_devices)
    picks = jnp.stack([first_q, first_q + row_devices], axis=1)
    sample_values = jnp.take_along_axis(samples, picks, axis=1)
    shard_of = picks // (samples.shape[1] // row_devices)
    offsets = sample_values - shard_of * shard_rows - processor_number * sub_rows
    both_halves = jnp.take(mixed, (offsets // 2) * row_devices + shard_of, axis=0)
    chosen = jnp.where(
        (offsets % 2 == 1)[:, :, None], both_halves[:, :, slab_width:], both_halves[:, :, :slab_width]
    )

    owner_list = owners[:, 0]
    preceding_rows = jnp.logical_and(
        owner_list[None, :] == owner_list[:, None], block_ids[None, :] < block_ids[:, None]
    )
    ranks = jnp.sum(preceding_rows.astype(jnp.int32), axis=1)
    slots = owner_list * CAPB + ranks
    placing = (jnp.arange(row_devices * CAPB, dtype=jnp.int32)[:, None] == slots[None, :]).astype(
        jnp.float32
    )
    bundled = jnp.einsum("kb,bps->kps", placing, chosen, precision=lax.Precision.HIGHEST)
    bundled = bundled.reshape(row_devices, CAPB, 2 * slab_width)
    arriving = lax.all_to_all(bundled, "rows", split_axis=0, concat_axis=0, tiled=True)
    received_rows = arriving.reshape(row_devices, CAPB, 2, slab_width).transpose(1, 3, 0, 2)
    received_rows = received_rows.reshape(CAPB, slab_width, row_devices * 2)
    other_rows = lax.ppermute(received_rows, "cols", [(0, 1), (1, 0)])
    owned_total = jnp.max(jnp.where(owner_list == processor_number, ranks + 1, 0))
    scalars = jnp.stack([lax.axis_index("cols").astype(jnp.int32), owned_total.astype(jnp.int32)])
    return cholesky_upper(scalars, received_rows, other_rows, slab_width)


def solution(mesh):
    in_specs = (P("cols", "rows"), P("rows"), P(), P())
    out_specs = P("rows", "cols", None)
    return jax.shard_map(
        per_device, mesh=mesh, in_specs=in_specs, out_specs=out_specs, check_vma=False
    )
```

```python
import math

import jax
import numpy as np
import jax.numpy as jnp
from jax import lax
from jax.experimental import pallas as pl
from jax.experimental.pallas import tpu as pltpu
from jax.sharding import PartitionSpec as P

HB = 128
SKETCH_ROW_COUNT = 256
CAPB = 4

PANEL = 32
STEP = 8


def cholesky_kernel(scalar_ref, own_ref, other_ref, out_ref, work_ref):
    blocks, width, samples = own_ref.shape
    order = 2 * width
    for b in range(blocks):
        first = jnp.where(scalar_ref[0] == 0, own_ref[b], other_ref[b])
        second = jnp.where(scalar_ref[0] == 0, other_ref[b], own_ref[b])
        columns = jnp.concatenate([first, second], axis=0)
        gram = lax.dot_general(
            columns, columns, (((1,), (1,)), ((), ())),
            precision=lax.Precision.HIGHEST, preferred_element_type=jnp.float32,
        ) / samples
        diagonal = (
            lax.broadcasted_iota(jnp.int32, (order, order), 0)
            == lax.broadcasted_iota(jnp.int32, (order, order), 1)
        )
        identity = jnp.where(diagonal, 1.0, 0.0)
        work_ref[b] = jnp.where(b < scalar_ref[1], gram, identity)
    lane = lax.broadcasted_iota(jnp.int32, (blocks, 1, order), 2)
    sub_panel = lax.broadcasted_iota(jnp.int32, (blocks, PANEL, order), 1)
    for p in range(order // PANEL):
        base = p * PANEL
        panel = work_ref[:, base:base + PANEL, :]
        for first in range(0, PANEL, STEP):
            columns = [
                jnp.broadcast_to(panel[:, :, base + first + m:base + first + m + 1], panel.shape)
                for m in range(STEP)
            ]
            factor_rows, factor_columns = [], []
            for m in range(STEP):
                jj = first + m
                column = columns[m]
                row = panel[:, jj:jj + 1, :]
                for earlier in range(m):
                    coupling = factor_columns[earlier][:, jj:jj + 1, :]
                    column = column - factor_columns[earlier] * coupling
                    row = row - coupling * factor_rows[earlier]
                inverse_root = lax.rsqrt(column[:, jj:jj + 1, :])
                factor_rows.append(jnp.where(lane >= base + jj, row * inverse_root, 0.0))
                factor_columns.append(jnp.where(sub_panel > jj, column * inverse_root, 0.0))
            for m in range(STEP):
                panel = panel - factor_columns[m] * factor_rows[m]
            for m in range(STEP):
                panel = jnp.where(sub_panel == first + m, factor_rows[m], panel)
        if p + 1 < order // PANEL:
            for b in range(blocks):
                update = lax.dot_general(
                    panel[b], panel[b], (((0,), (0,)), ((), ())),
                    precision=lax.Precision.HIGHEST, preferred_element_type=jnp.float32,
                )
                work_ref[b, base + PANEL:, :] = work_ref[b, base + PANEL:, :] - update[base + PANEL:, :]
        work_ref[:, base:base + PANEL, :] = panel
    start = pl.multiple_of(scalar_ref[0] * out_ref.shape[1], out_ref.shape[1])
    for b in range(blocks):
        out_ref[b] = jnp.where(b < scalar_ref[1], work_ref[b, pl.ds(start, out_ref.shape[1]), :], 0.0)


def cholesky_upper(scalars, own_rows, other_rows, slab_width):
    blocks, width, samples = own_rows.shape
    order = 2 * width
    return pl.pallas_call(
        cholesky_kernel,
        out_shape=jax.ShapeDtypeStruct((blocks, slab_width, order), jnp.float32),
        grid_spec=pltpu.PrefetchScalarGridSpec(
            num_scalar_prefetch=1,
            grid=(1,),
            in_specs=[pl.BlockSpec(memory_space=pltpu.VMEM)] * 2,
            out_specs=pl.BlockSpec(memory_space=pltpu.VMEM),
            scratch_shapes=[pltpu.VMEM((blocks, order, order), jnp.float32)],
        ),
    )(scalars, own_rows, other_rows)


def local_mix_kernel(matrix_ref, signs_ref, table_ref, out_ref):
    slab_width = matrix_ref.shape[0]
    rows = out_ref.shape[1]
    groups = table_ref.shape[0] // (2 * rows)

    def body(blk, carry):
        start = pl.multiple_of(blk * HB, HB)
        flips = (1 - 2 * signs_ref[:, pl.ds(start, HB)]).astype(jnp.float32)
        flipped = (matrix_ref[:, pl.ds(start, HB)].astype(jnp.float32) * flips).astype(jnp.bfloat16)
        mixed = lax.dot_general(
            table_ref[...], flipped, (((1,), (1,)), ((), ())),
            preferred_element_type=jnp.float32,
        )
        for parity in range(2):
            for h in range(groups):
                first = parity * groups * rows + h * rows
                out_ref[blk * groups + h, :, parity * slab_width:(parity + 1) * slab_width] = (
                    mixed[first:first + rows, :]
                )
        return carry

    lax.fori_loop(0, matrix_ref.shape[1] // HB, body, 0, unroll=True)


def local_mix(matrix, signs, table, row_devices):
    slab_width, shard_rows = matrix.shape
    sub_rows = shard_rows // row_devices
    return pl.pallas_call(
        local_mix_kernel,
        out_shape=jax.ShapeDtypeStruct((row_devices, sub_rows // 2, 2 * slab_width), jnp.float32),
        in_specs=[pl.BlockSpec(memory_space=pltpu.VMEM)] * 3,
        out_specs=pl.BlockSpec(memory_space=pltpu.VMEM),
    )(matrix, signs, table)


def walsh_sign_matrix(order):
    index_row = np.arange(order)
    parity = np.zeros((order, order), np.int64)
    for bit_place in range(order.bit_length() - 1):
        both = np.bitwise_and(index_row[:, None], index_row[None, :])
        parity = parity + np.bitwise_and(np.right_shift(both, bit_place), 1)
    return (1 - 2 * (parity % 2)).astype(np.float32)


def per_device(matrix, signs, samples, owners):
    slab_width = matrix.shape[0]
    shard_rows = matrix.shape[1]
    row_devices = lax.axis_size("rows")
    processor_number = lax.axis_index("rows")
    sub_rows = shard_rows // row_devices
    scale = 1.0 / math.sqrt(HB * row_devices)
    table = (walsh_sign_matrix(HB) * scale).reshape(HB // 2, 2, HB).transpose(1, 0, 2).reshape(HB, HB)
    outgoing = local_mix(matrix, signs.reshape(1, shard_rows), jnp.asarray(table, jnp.bfloat16), row_devices)
    received = lax.all_to_all(outgoing, "rows", split_axis=0, concat_axis=0, tiled=True)
    across = jnp.asarray(walsh_sign_matrix(row_devices))
    mixed = jnp.einsum(
        "st,tvl->vsl", across, received, precision=lax.Precision.HIGHEST
    ).reshape(row_devices * sub_rows // 2, 2 * slab_width)

    block_total = samples.shape[0]
    block_ids = jnp.arange(block_total, dtype=jnp.int32)
    first_q = jnp.mod(processor_number - block_ids, row_devices)
    picks = jnp.stack([first_q, first_q + row_devices], axis=1)
    sample_values = jnp.take_along_axis(samples, picks, axis=1)
    shard_of = picks // (samples.shape[1] // row_devices)
    offsets = sample_values - shard_of * shard_rows - processor_number * sub_rows
    both_halves = jnp.take(mixed, (offsets // 2) * row_devices + shard_of, axis=0)
    chosen = jnp.where(
        (offsets % 2 == 1)[:, :, None], both_halves[:, :, slab_width:], both_halves[:, :, :slab_width]
    )

    owner_list = owners[:, 0]
    preceding_rows = jnp.logical_and(
        owner_list[None, :] == owner_list[:, None], block_ids[None, :] < block_ids[:, None]
    )
    ranks = jnp.sum(preceding_rows.astype(jnp.int32), axis=1)
    slots = owner_list * CAPB + ranks
    placing = (jnp.arange(row_devices * CAPB, dtype=jnp.int32)[:, None] == slots[None, :]).astype(
        jnp.float32
    )
    bundled = jnp.einsum("kb,bps->kps", placing, chosen, precision=lax.Precision.HIGHEST)
    bundled = bundled.reshape(row_devices, CAPB, 2 * slab_width)
    owned_total = jnp.sum((owner_list == processor_number).astype(jnp.int32))
    scalars = jnp.stack([lax.axis_index("cols").astype(jnp.int32), owned_total.astype(jnp.int32)])
    bundled, scalars = lax.optimization_barrier((bundled, scalars))
    arriving = lax.all_to_all(bundled, "rows", split_axis=0, concat_axis=0, tiled=True)
    received_rows = arriving.reshape(row_devices, CAPB, 2, slab_width).transpose(1, 3, 0, 2)
    received_rows = received_rows.reshape(CAPB, slab_width, row_devices * 2)
    other_rows = lax.ppermute(received_rows, "cols", [(0, 1), (1, 0)])
    return cholesky_upper(scalars, received_rows, other_rows, slab_width)


def solution(mesh):
    in_specs = (P("cols", "rows"), P("rows"), P(), P())
    out_specs = P("rows", "cols", None)
    return jax.shard_map(
        per_device, mesh=mesh, in_specs=in_specs, out_specs=out_specs, check_vma=False
    )
```
